256 devices in a mesh: seq: 8 (over x, core), tensor: 32 (over z, y).
Axes of the slice: x: 4, y: 4, z: 8, core: 2. Of those that a mesh axis runs over, the one named last changes fastest.
Arguments:
- tokens: bfloat16 [2048, 2048], P(('seq', 'tensor')), may hold values from -6 to 6
- attn_gain: bfloat16 [2048], replicated, may hold values from 0.25 to 1.75
- w_qkv: bfloat16 [2048, 3, 2048], P(None, None, 'tensor'), may hold values from -0.125 to 0.125
- q_gain: bfloat16 [2048], P('tensor'), may hold values from 0.25 to 1.75
- k_gain: bfloat16 [2048], P('tensor'), may hold values from 0.25 to 1.75
- w_out: bfloat16 [2048, 2048], P('tensor'), may hold values from -0.125 to 0.125
- prefix_keys: bfloat16 [8, 2048, 2048], P('seq', None, 'tensor'), may hold values from -150 to 150
- prefix_values: bfloat16 [8, 2048, 2048], P('seq', None, 'tensor'), may hold values from -6 to 6
- segments: int32 [2048], replicated, may hold values from 0 to 31, never falling along the last dimension, each value on 1 to 256 neighbouring positions
- request_group: int32 [32], replicated, may hold values from 0 to 3
- prefix_owner: int32 [4], replicated, may hold values from 0 to 7, as said below
- mlp_gain: bfloat16 [2048], replicated, may hold values from 0.25 to 1.75
- expert_ids: int32 [2048, 8], P(('seq', 'tensor')), may hold values from 0 to 63, all different within a row; in each aligned block of 8 rows (0 to 7, 8 to 15, ...) at most 2 rows name the same one
- gate_weights: float32 [2048, 8], P(('seq', 'tensor')), may hold values from 0.05 to 0.5
- w_gate: bfloat16 [256, 2048, 256], P(('tensor', 'seq')), may hold values from -0.125 to 0.125
- w_up: bfloat16 [256, 2048, 256], P(('tensor', 'seq')), may hold values from -0.125 to 0.125
- w_down: bfloat16 [256, 256, 2048], P(('tensor', 'seq')), may hold values from -0.1875 to 0.1875
Outputs:
- output: bfloat16 [2048, 2048], P(('seq', 'tensor'))
- new_keys: bfloat16 [2048, 2048], P('seq', 'tensor')
- new_values: bfloat16 [2048, 2048], P('seq', 'tensor')
The draws below stay inside these ranges and needn't reach their ends.
Inputs may be any that keep to these rules, and one draw needn't show every extreme that they name: `segments`: each request's tokens are consecutive; a request has at most 256 tokens, and some request has exactly 256. `prefix_owner`: distinct slots. `expert_ids`: a token's experts are distinct; among the 8 rows of one device no expert is named more than 2 times, and that count is reached.
All inputs are finite; a program needn't handle non-finite values.
Results may differ from the reference program's by a relative error of at most 0.017.
Values may be sent and summed in bfloat16 or wider, within the bound.
No kernel may reach another device: no remote copies, remote signals or barrier semaphores. Data moves between devices by JAX's collectives and lax.ppermute only.
A program may use at most 64 MiB of HBM per device.

```python
import math
import jax
import jax.numpy as jnp
import numpy as np
from jax import lax

D = 2048
HEADS = 16
HD = 128
FF = 1024
TOP = 8
TOK_DEV = 8
PREFIX = 2048
EXPERTS = 64
UNITS = 256
TOK = 256
TOKENS = 2048
GROUPS = 4
REQS = 32
CAP = 2
N_SEQ = 8


def draw_prefix_keys(key, part):
    base = jax.random.normal(key, (N_SEQ, PREFIX, D), jnp.float32)
    return jnp.clip(base, -150.0, 150.0).astype(jnp.bfloat16)


def draw_prefix_owner(key, part):
    others = jax.random.permutation(jax.random.fold_in(key, 11), N_SEQ - 1)[:GROUPS - 1].astype(jnp.int32)
    chosen = jnp.concatenate([others, jnp.full((1,), N_SEQ - 1, jnp.int32)], axis=0)
    order = jax.random.permutation(jax.random.fold_in(key, 13), GROUPS)
    return chosen[order].astype(jnp.int32)


def plant(drawn, stream_key, smallest, high):
    place = [jax.random.randint(jax.random.fold_in(stream_key, axis), (), 0, length) for axis, length in enumerate(drawn.shape)]
    widest = drawn.shape.index(max(drawn.shape))
    next_to = place[:widest] + [(place[widest] + 1) % drawn.shape[widest]] + place[widest + 1:]
    return drawn.at[tuple(place)].set(smallest).at[tuple(next_to)].set(high)


def levels(rng, extent, cuts, least, top_value):
    def one(dim, blocks):
        steps = jax.random.uniform(jax.random.fold_in(jax.random.fold_in(rng, 6), dim), (blocks,), jnp.float32, least / len(cuts), top_value / len(cuts))
        return jnp.repeat(jnp.exp(steps), extent[dim] // blocks).reshape((-1,) + (1,) * (len(extent) - dim - 1))

    factor_of = one(*cuts[0])
    for cut in cuts[1:]:
        factor_of = factor_of * one(*cut)
    return factor_of


def split_up(number_of, total, bound, lean):
    weights = [(1 << 20) // math.isqrt(grade ** lean) + 1 for grade in range(2, number_of + 1)]
    rest, given = total - bound - (number_of - 1), [1] * (number_of - 1)
    while rest > 0:
        free = [i for i in range(number_of - 1) if given[i] < bound]
        mass, budget = sum([weights[i] for i in free]), rest
        for i in free:
            extra = min(bound - given[i], max(1, budget * weights[i] // mass), rest)
            given[i] = given[i] + extra
            rest = rest - extra
    return np.array([bound] + given)


def uneven(rng, count, total, most, lean):
    if count == 2:
        one = jax.random.randint(rng, (), max(1, total - most), min(most, total - 1) + 1)
        return jnp.stack([one, total - one])
    sizes = jnp.asarray(split_up(count, total, most, lean), jnp.int32)
    couples = (count - 1) // 2
    donor, taker = sizes[1:1 + 2 * couples:2], sizes[2:2 + 2 * couples:2]
    slack = jnp.minimum(donor - 1, most - taker)
    moved = jax.random.randint(jax.random.fold_in(rng, 1), (couples,), 0, 1 << 20) % (slack + 1)
    sizes = sizes.at[1:1 + 2 * couples:2].set(donor - moved).at[2:2 + 2 * couples:2].set(taker + moved)
    return sizes[jax.random.permutation(jax.random.fold_in(rng, 2), count)]


def assign_block(own_key, own, number, rows, number_of, top, limit, slope):
    sequence = jax.random.permutation(own_key, number_of)
    crowded, ordinary = portions_of(number_of, rows * top, limit, slope, True), portions_of(number_of, rows * top, limit, slope, False)
    places = jnp.arange(number_of)

    def named(sizes, turn):
        used = int((sizes > 0).sum())
        fixed = max(1, used // 4)
        shifted = fixed + (places - fixed + turn * (used - fixed)) % max(1, number_of - fixed)
        return jnp.zeros((number_of,), jnp.int32).at[sequence[jnp.where(places < fixed, places, shifted)]].set(jnp.asarray(sizes, jnp.int32))

    sizes = jnp.where(number % 4 == 0, named(crowded, number // 4), named(ordinary, number - number // 4 - 1))
    mixed = jax.random.permutation(jax.random.fold_in(own, 3), number_of)
    source_of, taker = mixed[0:number_of // 2 * 2:2], mixed[1:number_of // 2 * 2:2]
    room = jnp.minimum(sizes[source_of] - 1, limit - sizes[taker]) // 2
    room = jnp.where((source_of == sequence[0]) | (taker == sequence[0]) | (sizes[taker] == 0), 0, jnp.maximum(room, 0))
    shifted = jax.random.randint(jax.random.fold_in(own, 4), (number_of // 2,), 0, 1 << 20) % (room + 1)
    sizes = sizes.at[source_of].add(-shifted).at[taker].add(shifted)
    items = jnp.searchsorted(jnp.cumsum(sizes), jnp.arange(rows * top), side="right").astype(jnp.int32)
    table = items.reshape(top, rows).T
    table = table[jax.random.permutation(jax.random.fold_in(own, 1), rows)]
    turn = jax.random.randint(jax.random.fold_in(own, 2), (rows, 1), 0, top)
    return jnp.take_along_axis(table, (jnp.arange(top)[None, :] + turn) % top, axis=1)


def portions_of(number_of, total, reach, lean, full):
    portions = [(1 << 20) // math.isqrt(standing ** lean) + 1 for standing in range(1, number_of + 1)]
    largest = reach if full else min(reach, max(-(-total // number_of), total * portions[0] // sum(portions)))
    least = 1 if total - largest >= number_of - 1 else 0
    holding, rest = [largest] + [least] * (number_of - 1), total - largest - least * (number_of - 1)
    while rest > 0:
        candidates = [i for i in range(1, number_of) if holding[i] < largest] or [i for i in range(1, number_of) if holding[i] < reach]
        mass, remaining = sum([portions[i] for i in candidates]), rest
        for i in candidates:
            addition = min(reach - holding[i], max(1, remaining * portions[i] // mass), rest)
            holding[i] = holding[i] + addition
            rest = rest - addition
    return np.array(holding)


def normal_values(stream_key, extent, deviation, bound, shards=(), kind=jnp.bfloat16):
    values = jax.random.normal(stream_key, extent, jnp.float32) * deviation
    if len(shards) > 0:
        values = levels(stream_key, extent, shards, -0.22, 0.18) * values
    return jnp.clip(values, min=-bound, max=bound).astype(kind)


def setup_inputs(seed: int = 0) -> dict:
    streams_of = jax.random.split(jax.random.key(seed), 18)
    tokens = normal_values(streams_of[0], (TOKENS, D), 1.0, 6.0, ((0, 256),))
    attn_gain = jnp.clip(1.0 + 0.15 * jax.random.normal(streams_of[1], (D,), jnp.float32), 0.25, 1.75).astype(jnp.bfloat16)
    w_qkv = normal_values(streams_of[2], (D, 3, D), D ** -0.5, 0.125, ((2, 32),))
    q_gain = jnp.clip(1.0 + 0.15 * jax.random.normal(streams_of[3], (D,), jnp.float32), 0.25, 1.75).astype(jnp.bfloat16)
    k_gain = jnp.clip(1.0 + 0.15 * jax.random.normal(streams_of[4], (D,), jnp.float32), 0.25, 1.75).astype(jnp.bfloat16)
    w_out = normal_values(streams_of[5], (D, D), D ** -0.5, 0.125, ((0, 32),))
    prefix_keys = draw_prefix_keys(jax.random.fold_in(streams_of[17], 71), 0)
    prefix_values = normal_values(streams_of[7], (N_SEQ, PREFIX, D), 1.0, 6.0, ((0, 8), (2, 32)))
    segments = jnp.searchsorted(jnp.cumsum(uneven(streams_of[8], REQS, TOKENS, TOK, 2)), jnp.arange(TOKENS), side="right").astype(jnp.int32)
    request_group = plant(jax.random.randint(streams_of[9], (REQS,), 0, GROUPS), jax.random.fold_in(streams_of[9], 1), 0, GROUPS - 1).astype(jnp.int32)
    prefix_owner = draw_prefix_owner(jax.random.fold_in(streams_of[17], 71), 0)
    mlp_gain = jnp.clip(1.0 + 0.15 * jax.random.normal(streams_of[11], (D,), jnp.float32), 0.25, 1.75).astype(jnp.bfloat16)
    expert_ids_keys = jax.random.split(jax.random.fold_in(streams_of[12], 1), TOKENS // TOK_DEV)
    expert_ids_turns = jax.random.permutation(jax.random.fold_in(streams_of[12], 3), TOKENS // TOK_DEV)
    expert_ids = jax.vmap(lambda own, number: assign_block(jax.random.fold_in(streams_of[12], 2), own, number, TOK_DEV, EXPERTS, TOP, CAP, 2))(expert_ids_keys, expert_ids_turns).reshape((TOKENS, TOP))
    gate_weights = jnp.clip(jnp.exp(math.log(0.5) - 2.3025851 * jax.random.uniform(streams_of[13], (TOKENS, TOP), jnp.float32) ** levels(streams_of[13], (TOKENS, TOP), ((0, 256),), -0.2, 0.2)), 0.05, 0.5)
    w_gate = normal_values(streams_of[14], (EXPERTS * FF // UNITS, D, UNITS), D ** -0.5, 0.125, ((0, 256),))
    w_up = normal_values(streams_of[15], (EXPERTS * FF // UNITS, D, UNITS), D ** -0.5, 0.125, ((0, 256),))
    w_down = normal_values(streams_of[16], (EXPERTS * FF // UNITS, UNITS, D), FF ** -0.5, 0.1875, ((0, 256),))
    return dict(tokens=tokens, attn_gain=attn_gain, w_qkv=w_qkv, q_gain=q_gain, k_gain=k_gain, w_out=w_out, prefix_keys=prefix_keys, prefix_values=prefix_values, segments=segments, request_group=request_group, prefix_owner=prefix_owner, mlp_gain=mlp_gain, expert_ids=expert_ids, gate_weights=gate_weights, w_gate=w_gate, w_up=w_up, w_down=w_down)


def rms_scale(values, gain):
    mean_square = lax.optimization_barrier(jnp.mean(values * values, axis=-1, keepdims=True))
    return values * lax.rsqrt(mean_square + 1e-05) * gain.astype(jnp.float32)

def reference(tokens, attn_gain, w_qkv, q_gain, k_gain, w_out, prefix_keys, prefix_values, segments, request_group, prefix_owner, mlp_gain, expert_ids, gate_weights, w_gate, w_up, w_down):
    quarters = FF // UNITS
    gate_full = jnp.transpose(w_gate.reshape(EXPERTS, quarters, D, UNITS), (0, 2, 1, 3)).reshape(EXPERTS, D, FF)
    up_full = jnp.transpose(w_up.reshape(EXPERTS, quarters, D, UNITS), (0, 2, 1, 3)).reshape(EXPERTS, D, FF)
    down_full = w_down.reshape(EXPERTS, FF, D)
    tokens_wide = tokens.astype(jnp.float32)
    normed = rms_scale(tokens_wide, attn_gain).astype(jnp.bfloat16)
    projected = jnp.dot(normed, w_qkv.reshape(D, 3 * D), preferred_element_type=jnp.float32).reshape(TOKENS, 3, D)
    queries = rms_scale(projected[:, 0], q_gain).astype(jnp.bfloat16)
    new_keys = rms_scale(projected[:, 1], k_gain).astype(jnp.bfloat16)
    new_values = projected[:, 2].astype(jnp.bfloat16)
    token_group = request_group[segments]
    all_keys = jnp.concatenate([prefix_keys[prefix_owner[group]] for group in range(GROUPS)] + [new_keys], axis=0)
    all_values = jnp.concatenate([prefix_values[prefix_owner[group]] for group in range(GROUPS)] + [new_values], axis=0)
    key_group = jnp.repeat(jnp.arange(GROUPS, dtype=jnp.int32), PREFIX)
    keys_wide = all_keys.astype(jnp.float32).reshape(-1, HEADS, HD)
    values_wide = all_values.astype(jnp.float32).reshape(-1, HEADS, HD)
    positions = jnp.arange(TOKENS, dtype=jnp.int32)

    def attend(block_start):
        block_queries = lax.dynamic_slice_in_dim(queries, block_start, TOK, 0).astype(jnp.float32).reshape(TOK, HEADS, HD)
        block_seg = lax.dynamic_slice_in_dim(segments, block_start, TOK, 0)
        block_group = lax.dynamic_slice_in_dim(token_group, block_start, TOK, 0)
        block_pos = block_start + jnp.arange(TOK, dtype=jnp.int32)
        prefix_mask = block_group[:, None] == key_group[None, :]
        suffix_mask = (block_seg[:, None] == segments[None, :]) & (positions[None, :] <= block_pos[:, None])
        mask = jnp.concatenate([prefix_mask, suffix_mask], axis=1)
        scores = jnp.einsum('qhd,khd->hqk', block_queries, keys_wide, precision=lax.Precision.HIGHEST) * HD ** (-0.5)
        scores = jnp.where(mask[None], scores, -1e+30)
        largest = lax.optimization_barrier(jnp.max(scores, axis=-1, keepdims=True))
        weights = jnp.where(mask[None], jnp.exp(scores - largest), 0.0)
        total = lax.optimization_barrier(jnp.sum(weights, axis=-1))
        rounded = lax.optimization_barrier(weights.astype(jnp.bfloat16))
        mixed = jnp.einsum('hqk,khd->qhd', rounded.astype(jnp.float32), values_wide, precision=lax.Precision.HIGHEST)
        mixed = mixed / jnp.transpose(total)[:, :, None]
        return mixed.astype(jnp.bfloat16).reshape(TOK, D)
    starts = jnp.arange(TOKENS // TOK, dtype=jnp.int32) * TOK
    attended = lax.map(attend, starts).reshape(TOKENS, D)
    attn_sum = jnp.dot(attended, w_out, preferred_element_type=jnp.float32)
    mixed_rows = (tokens_wide + attn_sum).astype(jnp.bfloat16)
    expert_in = rms_scale(mixed_rows.astype(jnp.float32), mlp_gain).astype(jnp.bfloat16)
    blocks = TOKENS // TOK_DEV
    ids_block = expert_ids.reshape(blocks, TOK_DEV * TOP)
    gates_block = gate_weights.reshape(blocks, TOK_DEV * TOP).astype(jnp.float32)
    onehot = (ids_block[:, :, None] == jnp.arange(EXPERTS, dtype=jnp.int32)[None, None, :]).astype(jnp.int32)
    before = jnp.cumsum(onehot, axis=1) - onehot
    position = lax.optimization_barrier(jnp.sum(before * onehot, axis=-1))
    slot = (ids_block * CAP + position).astype(jnp.int32)
    block_rows = jnp.arange(blocks, dtype=jnp.int32)[:, None]
    token_index = (block_rows * TOK_DEV + jnp.arange(TOK_DEV * TOP, dtype=jnp.int32)[None, :] // TOP).astype(jnp.int32)
    token_of_slot = jnp.zeros((blocks, EXPERTS * CAP), jnp.int32).at[block_rows, slot].set(token_index)
    weight_of_slot = jnp.zeros((blocks, EXPERTS * CAP), jnp.float32).at[block_rows, slot].set(gates_block)

    def run_expert(moe_sum, inputs):
        gate_matrix, up_matrix, down_matrix, expert = inputs
        rows = lax.dynamic_slice_in_dim(token_of_slot, expert * CAP, CAP, 1).reshape(-1)
        scale = lax.dynamic_slice_in_dim(weight_of_slot, expert * CAP, CAP, 1).reshape(-1)
        picked = expert_in[rows]
        gated = jnp.dot(picked, gate_matrix, preferred_element_type=jnp.float32)
        upward = jnp.dot(picked, up_matrix, preferred_element_type=jnp.float32)
        activity = (jax.nn.silu(gated) * upward).astype(jnp.bfloat16)
        result = jnp.dot(activity, down_matrix, preferred_element_type=jnp.float32)
        return (moe_sum.at[rows].add(result * scale[:, None]), None)
    moe_init = jnp.zeros((TOKENS, D), jnp.float32)
    moe_sum, _ = lax.scan(run_expert, moe_init, (gate_full, up_full, down_full, jnp.arange(EXPERTS, dtype=jnp.int32)))
    output = (mixed_rows.astype(jnp.float32) + moe_sum).astype(jnp.bfloat16)
    return (output, new_keys, new_values)
```

```python
import jax
import jax.numpy as jnp
from jax import lax
from jax.sharding import PartitionSpec as P

HD = 128
TOP = 8
EXP_DEV = 2


def from_partner(value, axis, stride):
    mask = 2**stride
    pairs = [(source, source ^ mask) for source in range(lax.axis_size(axis))]
    return lax.ppermute(value, axis, pairs)


def passed_along(value, axis, by):
    devices = lax.axis_size(axis)
    pairs = [(i, i + by) for i in range(devices) if 0 <= i + by < devices]
    return lax.ppermute(value, axis, pairs)


def gather_by_exchange(value, axis):
    devices = lax.axis_size(axis)
    copies = jnp.broadcast_to(value[None], (devices,) + value.shape)
    got = lax.all_to_all(copies, axis, 0, 0, tiled=True)
    return got


def rms_scale(values, gain):
    mean_square = jnp.mean(values * values, axis=-1, keepdims=True)
    return values * lax.rsqrt(mean_square + 1e-05) * gain.astype(jnp.float32)


def attend_block(carry, queries_heads, block, mask):
    largest, total, accum = carry
    heads_local = queries_heads.shape[1]
    count = block.shape[0]
    key_block = block[:, 0].reshape(count, heads_local, HD)
    value_block = block[:, 1].reshape(count, heads_local, HD)
    scores = jnp.einsum(
        "qhd,khd->hqk", queries_heads, key_block, preferred_element_type=jnp.float32
    ) * HD ** (-0.5)
    scores = jnp.where(mask[None], scores, -1e30)
    new_largest = jnp.maximum(largest, jnp.max(scores, axis=-1))
    weights = jnp.where(mask[None], jnp.exp(scores - new_largest[:, :, None]), 0.0)
    factor = jnp.exp(largest - new_largest)
    total = total * factor + jnp.sum(weights, axis=-1)
    update = jnp.einsum(
        "hqk,khd->hqd",
        weights.astype(jnp.bfloat16),
        value_block,
        preferred_element_type=jnp.float32,
    )
    accum = accum * factor[:, :, None] + update
    return (new_largest, total, accum)


def local(
    tokens,
    attn_gain,
    w_qkv,
    q_gain,
    k_gain,
    w_out,
    prefix_keys,
    prefix_values,
    segments,
    request_group,
    prefix_owner,
    mlp_gain,
    expert_ids,
    gate_weights,
    w_gate,
    w_up,
    w_down,
):
    tensor_size = lax.axis_size("tensor")
    seq_size = lax.axis_size("seq")
    seq_index = lax.axis_index("seq")
    tensor_index = lax.axis_index("tensor")
    tok_dev = tokens.shape[0]
    width = tokens.shape[1]
    tok_seq = tok_dev * tensor_size
    columns = w_qkv.shape[2]
    normed = rms_scale(tokens.astype(jnp.float32), attn_gain).astype(jnp.bfloat16)
    w_flat = w_qkv.reshape(width, 3 * columns)
    projected = jnp.dot(
        gather_by_exchange(normed, "tensor").reshape(tok_seq, width),
        w_flat,
        preferred_element_type=jnp.float32,
    )
    query_part = projected[:, :columns]
    key_part = projected[:, columns : 2 * columns]
    partial_squares = jnp.stack(
        [jnp.sum(query_part * query_part, axis=-1), jnp.sum(key_part * key_part, axis=-1)]
    )
    squares = jnp.sum(gather_by_exchange(partial_squares, "tensor"), axis=0)
    query_rows = (
        query_part * lax.rsqrt(squares[0] / width + 1e-05)[:, None] * q_gain.astype(jnp.float32)
    ).astype(jnp.bfloat16)
    new_keys = (
        key_part * lax.rsqrt(squares[1] / width + 1e-05)[:, None] * k_gain.astype(jnp.float32)
    ).astype(jnp.bfloat16)
    new_values = projected[:, 2 * columns :].astype(jnp.bfloat16)
    stacked = jnp.stack(
        [
            jnp.concatenate([new_keys, prefix_keys[0]], axis=0),
            jnp.concatenate([new_values, prefix_values[0]], axis=0),
        ],
        axis=1,
    )
    half_rows = tok_seq // 2
    lower_bit = tensor_index % 2
    partner = from_partner(stacked, "tensor", 0)
    full = jnp.where(
        lower_bit == 0,
        jnp.concatenate([stacked, partner], axis=-1),
        jnp.concatenate([partner, stacked], axis=-1),
    )
    query_halves = query_rows.reshape(2, half_rows, columns)
    own_half = lax.dynamic_index_in_dim(query_halves, lower_bit, 0, keepdims=False)
    send_half = lax.dynamic_index_in_dim(query_halves, 1 - lower_bit, 0, keepdims=False)
    got_half = from_partner(send_half, "tensor", 0)
    query_full = jnp.where(
        lower_bit == 0,
        jnp.concatenate([own_half, got_half], axis=-1),
        jnp.concatenate([got_half, own_half], axis=-1),
    )
    query_offset = lower_bit * half_rows
    heads_local = 1
    suffix_full = full[:tok_seq]
    prefix_full = full[tok_seq:]
    queries_heads = query_full.reshape(half_rows, heads_local, HD)
    groups_count = prefix_owner.shape[0]
    request_count = request_group.shape[0]
    token_group = jnp.sum(
        jnp.where(
            segments[:, None] == jnp.arange(request_count, dtype=jnp.int32)[None, :],
            request_group[None, :],
            0,
        ),
        axis=1,
    )
    base_row = seq_index * tok_seq
    query_start = base_row + query_offset
    query_seg = lax.dynamic_slice_in_dim(segments, query_start, half_rows, 0)
    query_group = lax.dynamic_slice_in_dim(token_group, query_start, half_rows, 0)
    query_pos = query_start + jnp.arange(half_rows, dtype=jnp.int32)
    padded_seg = jnp.concatenate([jnp.full((tok_seq,), -1, jnp.int32), segments], axis=0)
    key_seg = lax.dynamic_slice_in_dim(padded_seg, base_row, 2 * tok_seq, 0)
    key_pos = base_row - tok_seq + jnp.arange(2 * tok_seq, dtype=jnp.int32)
    previous = passed_along(suffix_full, "seq", 1)
    suffix_keys = jnp.concatenate([previous, suffix_full], axis=0)
    suffix_mask = (key_seg[None, :] == query_seg[:, None]) & (
        key_pos[None, :] <= query_pos[:, None]
    )
    carry = (
        jnp.full((heads_local, half_rows), -1e30, jnp.float32),
        jnp.zeros((heads_local, half_rows), jnp.float32),
        jnp.zeros((heads_local, half_rows, HD), jnp.float32),
    )
    carry = attend_block(carry, queries_heads, suffix_keys, suffix_mask)
    owner_of_query = jnp.sum(
        jnp.where(
            query_group[:, None] == jnp.arange(groups_count, dtype=jnp.int32)[None, :],
            prefix_owner[None, :],
            0,
        ),
        axis=1,
    )
    state = carry
    piece = lax.all_gather(prefix_full[None], "seq", axis=0, tiled=True)
    start = jnp.int32(0)
    for offset in range(piece.shape[0]):
        slot_mask = (owner_of_query == start + offset)[:, None]
        state = attend_block(state, queries_heads, piece[offset], slot_mask)
    carry = state
    attended = (carry[2] / carry[1][:, :, None]).astype(jnp.bfloat16)
    attended = jnp.transpose(attended, (1, 0, 2)).reshape(half_rows, heads_local * HD)
    split_out = attended.reshape(half_rows, 2, columns)
    own_out = lax.dynamic_index_in_dim(split_out, lower_bit, 1, keepdims=False)
    send_out = lax.dynamic_index_in_dim(split_out, 1 - lower_bit, 1, keepdims=False)
    got_out = from_partner(send_out, "tensor", 0)
    attended_local = jnp.where(
        lower_bit == 0,
        jnp.concatenate([own_out, got_out], axis=0),
        jnp.concatenate([got_out, own_out], axis=0),
    )
    attn_partial = jnp.dot(attended_local, w_out, preferred_element_type=jnp.float32)
    attn_partial = attn_partial.astype(jnp.bfloat16).reshape(tensor_size, tok_dev, width)
    attn_sum = jnp.sum(
        lax.all_to_all(attn_partial, "tensor", 0, 0, tiled=True).astype(jnp.float32), axis=0
    )
    mixed_rows = (tokens.astype(jnp.float32) + attn_sum).astype(jnp.bfloat16)
    expert_in = rms_scale(mixed_rows.astype(jnp.float32), mlp_gain).astype(jnp.bfloat16)
    exp_local = EXP_DEV
    experts_all = exp_local * tensor_size
    own_expert = seq_index // (seq_size // exp_local)
    capacity = max(2, 2 * tok_dev * TOP // experts_all)
    flat_ids = expert_ids.reshape(-1)
    onehot = (flat_ids[:, None] == jnp.arange(experts_all, dtype=jnp.int32)[None, :]).astype(
        jnp.int32
    )
    before = jnp.cumsum(onehot, axis=0) - onehot
    slot = flat_ids * capacity + jnp.sum(before * onehot, axis=1)
    slot_match = (
        slot.reshape(tok_dev, TOP)[:, :, None]
        == jnp.arange(experts_all * capacity, dtype=jnp.int32)[None, None, :]
    )
    dispatch_table = jnp.transpose(jnp.any(slot_match, axis=1)).astype(jnp.bfloat16)
    combine_table = jnp.sum(jnp.where(slot_match, gate_weights[:, :, None], 0.0), axis=1)
    buffer = jnp.dot(dispatch_table, expert_in, preferred_element_type=jnp.float32).astype(
        jnp.bfloat16
    )
    buffer = buffer.reshape(tensor_size, exp_local, capacity, width)
    received = lax.all_to_all(buffer, "tensor", split_axis=0, concat_axis=0, tiled=True)
    gate_local = w_gate[0]
    up_local = w_up[0]
    down_local = w_down[0]
    keep_expert = (jnp.arange(exp_local, dtype=jnp.int32) == own_expert)[None, None, :, None, None]
    chosen = lax.dynamic_index_in_dim(
        lax.all_gather(received[None], "seq", axis=0, tiled=True), own_expert, 2, keepdims=False
    )
    gated = jnp.einsum("srcd,df->srcf", chosen, gate_local, preferred_element_type=jnp.float32)
    upward = jnp.einsum("srcd,df->srcf", chosen, up_local, preferred_element_type=jnp.float32)
    activity = (jax.nn.silu(gated) * upward).astype(jnp.bfloat16)
    result = jnp.einsum("srcf,fd->srcd", activity, down_local, preferred_element_type=jnp.float32)
    partials = jnp.where(keep_expert, result[:, :, None], 0.0)
    summed = lax.psum_scatter(
        partials.astype(jnp.bfloat16), "seq", scatter_dimension=0, tiled=True
    ).astype(jnp.float32)
    returned = lax.all_to_all(
        summed[0].astype(jnp.bfloat16), "tensor", split_axis=0, concat_axis=0, tiled=True
    ).astype(jnp.float32)
    moe_sum = jnp.dot(
        combine_table,
        returned.reshape(experts_all * capacity, width),
        preferred_element_type=jnp.float32,
        precision=lax.Precision.HIGHEST,
    )
    output = (mixed_rows.astype(jnp.float32) + moe_sum).astype(jnp.bfloat16)
    return (output, new_keys, new_values)


def solution(mesh):
    return jax.shard_map(
        local,
        mesh=mesh,
        in_specs=(
            P(("seq", "tensor"), None),
            P(),
            P(None, None, "tensor"),
            P("tensor"),
            P("tensor"),
            P("tensor", None),
            P("seq", None, "tensor"),
            P("seq", None, "tensor"),
            P(),
            P(),
            P(),
            P(),
            P(("seq", "tensor"), None),
            P(("seq", "tensor"), None),
            P(("tensor", "seq"), None, None),
            P(("tensor", "seq"), None, None),
            P(("tensor", "seq"), None, None),
        ),
        out_specs=(P(("seq", "tensor"), None), P("seq", "tensor"), P("seq", "tensor")),
        check_vma=False,
    )
```

```python
import jax
import jax.numpy as jnp
from jax import lax
from jax.sharding import PartitionSpec as P

HD = 128
TOP = 8
EXP_DEV = 2


def from_partner(value, axis, stride):
    mask = 2**stride
    pairs = [(source, source ^ mask) for source in range(lax.axis_size(axis))]
    return lax.ppermute(value, axis, pairs)


def passed_along(value, axis, by):
    devices = lax.axis_size(axis)
    pairs = [(i, i + by) for i in range(devices) if 0 <= i + by < devices]
    return lax.ppermute(value, axis, pairs)


def gather_by_exchange(value, axis):
    devices = lax.axis_size(axis)
    copies = jnp.broadcast_to(value[None], (devices,) + value.shape)
    got = lax.all_to_all(copies, axis, 0, 0, tiled=True)
    return got


def rms_scale(values, gain):
    mean_square = jnp.mean(values * values, axis=-1, keepdims=True)
    return values * lax.rsqrt(mean_square + 1e-05) * gain.astype(jnp.float32)


def attend_block(carry, queries_heads, block, mask):
    largest, total, accum = carry
    heads_local = queries_heads.shape[1]
    count = block.shape[0]
    key_block = block[:, 0].reshape(count, heads_local, HD)
    value_block = block[:, 1].reshape(count, heads_local, HD)
    scores = jnp.einsum(
        "qhd,khd->hqk", queries_heads, key_block, preferred_element_type=jnp.float32
    ) * HD ** (-0.5)
    scores = jnp.where(mask[None], scores, -1e30)
    new_largest = jnp.maximum(largest, jnp.max(scores, axis=-1))
    weights = jnp.where(mask[None], jnp.exp(scores - new_largest[:, :, None]), 0.0)
    factor = jnp.exp(largest - new_largest)
    total = total * factor + jnp.sum(weights, axis=-1)
    update = jnp.einsum(
        "hqk,khd->hqd",
        weights.astype(jnp.bfloat16),
        value_block,
        preferred_element_type=jnp.float32,
    )
    accum = accum * factor[:, :, None] + update
    return (new_largest, total, accum)


def local(
    tokens,
    attn_gain,
    w_qkv,
    q_gain,
    k_gain,
    w_out,
    prefix_keys,
    prefix_values,
    segments,
    request_group,
    prefix_owner,
    mlp_gain,
    expert_ids,
    gate_weights,
    w_gate,
    w_up,
    w_down,
):
    tensor_size = lax.axis_size("tensor")
    seq_size = lax.axis_size("seq")
    seq_index = lax.axis_index("seq")
    tensor_index = lax.axis_index("tensor")
    tok_dev = tokens.shape[0]
    width = tokens.shape[1]
    tok_seq = tok_dev * tensor_size
    columns = w_qkv.shape[2]
    lower_bit = tensor_index % 2
    prefix_own = jnp.stack([prefix_keys[0], prefix_values[0]], axis=1)
    prefix_partner = from_partner(prefix_own, "tensor", 0)
    prefix_full = jnp.where(
        lower_bit == 0,
        jnp.concatenate([prefix_own, prefix_partner], axis=-1),
        jnp.concatenate([prefix_partner, prefix_own], axis=-1),
    )
    piece = lax.all_gather(prefix_full[None], "seq", axis=0, tiled=True)
    normed = rms_scale(tokens.astype(jnp.float32), attn_gain).astype(jnp.bfloat16)
    w_flat = w_qkv.reshape(width, 3 * columns)
    projected = jnp.dot(
        gather_by_exchange(normed, "tensor").reshape(tok_seq, width),
        w_flat,
        preferred_element_type=jnp.float32,
    )
    query_part = projected[:, :columns]
    key_part = projected[:, columns : 2 * columns]
    partial_squares = jnp.stack(
        [jnp.sum(query_part * query_part, axis=-1), jnp.sum(key_part * key_part, axis=-1)]
    )
    squares = jnp.sum(gather_by_exchange(partial_squares, "tensor"), axis=0)
    query_rows = (
        query_part * lax.rsqrt(squares[0] / width + 1e-05)[:, None] * q_gain.astype(jnp.float32)
    ).astype(jnp.bfloat16)
    new_keys = (
        key_part * lax.rsqrt(squares[1] / width + 1e-05)[:, None] * k_gain.astype(jnp.float32)
    ).astype(jnp.bfloat16)
    new_values = projected[:, 2 * columns :].astype(jnp.bfloat16)
    stacked = jnp.stack([new_keys, new_values], axis=1)
    half_rows = tok_seq // 2
    partner = from_partner(stacked, "tensor", 0)
    suffix_full = jnp.where(
        lower_bit == 0,
        jnp.concatenate([stacked, partner], axis=-1),
        jnp.concatenate([partner, stacked], axis=-1),
    )
    query_halves = query_rows.reshape(2, half_rows, columns)
    own_half = lax.dynamic_index_in_dim(query_halves, lower_bit, 0, keepdims=False)
    send_half = lax.dynamic_index_in_dim(query_halves, 1 - lower_bit, 0, keepdims=False)
    got_half = from_partner(send_half, "tensor", 0)
    query_full = jnp.where(
        lower_bit == 0,
        jnp.concatenate([own_half, got_half], axis=-1),
        jnp.concatenate([got_half, own_half], axis=-1),
    )
    query_offset = lower_bit * half_rows
    heads_local = 1
    queries_heads = query_full.reshape(half_rows, heads_local, HD)
    groups_count = prefix_owner.shape[0]
    request_count = request_group.shape[0]
    token_group = jnp.sum(
        jnp.where(
            segments[:, None] == jnp.arange(request_count, dtype=jnp.int32)[None, :],
            request_group[None, :],
            0,
        ),
        axis=1,
    )
    base_row = seq_index * tok_seq
    query_start = base_row + query_offset
    query_seg = lax.dynamic_slice_in_dim(segments, query_start, half_rows, 0)
    query_group = lax.dynamic_slice_in_dim(token_group, query_start, half_rows, 0)
    query_pos = query_start + jnp.arange(half_rows, dtype=jnp.int32)
    padded_seg = jnp.concatenate([jnp.full((tok_seq,), -1, jnp.int32), segments], axis=0)
    key_seg = lax.dynamic_slice_in_dim(padded_seg, base_row, 2 * tok_seq, 0)
    key_pos = base_row - tok_seq + jnp.arange(2 * tok_seq, dtype=jnp.int32)
    previous = passed_along(suffix_full, "seq", 1)
    suffix_keys = jnp.concatenate([previous, suffix_full], axis=0)
    suffix_mask = (key_seg[None, :] == query_seg[:, None]) & (
        key_pos[None, :] <= query_pos[:, None]
    )
    carry = (
        jnp.full((heads_local, half_rows), -1e30, jnp.float32),
        jnp.zeros((heads_local, half_rows), jnp.float32),
        jnp.zeros((heads_local, half_rows, HD), jnp.float32),
    )
    carry = attend_block(carry, queries_heads, suffix_keys, suffix_mask)
    owner_of_query = jnp.sum(
        jnp.where(
            query_group[:, None] == jnp.arange(groups_count, dtype=jnp.int32)[None, :],
            prefix_owner[None, :],
            0,
        ),
        axis=1,
    )
    state = carry
    start = jnp.int32(0)
    for offset in range(piece.shape[0]):
        slot_mask = (owner_of_query == start + offset)[:, None]
        state = attend_block(state, queries_heads, piece[offset], slot_mask)
    carry = state
    attended = (carry[2] / carry[1][:, :, None]).astype(jnp.bfloat16)
    attended = jnp.transpose(attended, (1, 0, 2)).reshape(half_rows, heads_local * HD)
    split_out = attended.reshape(half_rows, 2, columns)
    own_out = lax.dynamic_index_in_dim(split_out, lower_bit, 1, keepdims=False)
    send_out = lax.dynamic_index_in_dim(split_out, 1 - lower_bit, 1, keepdims=False)
    got_out = from_partner(send_out, "tensor", 0)
    attended_local = jnp.where(
        lower_bit == 0,
        jnp.concatenate([own_out, got_out], axis=0),
        jnp.concatenate([got_out, own_out], axis=0),
    )
    attn_partial = jnp.dot(attended_local, w_out, preferred_element_type=jnp.float32)
    attn_partial = attn_partial.astype(jnp.bfloat16).reshape(tensor_size, tok_dev, width)
    attn_sum = jnp.sum(
        lax.all_to_all(attn_partial, "tensor", 0, 0, tiled=True).astype(jnp.float32), axis=0
    )
    mixed_rows = (tokens.astype(jnp.float32) + attn_sum).astype(jnp.bfloat16)
    expert_in = rms_scale(mixed_rows.astype(jnp.float32), mlp_gain).astype(jnp.bfloat16)
    exp_local = EXP_DEV
    experts_all = exp_local * tensor_size
    own_expert = seq_index // (seq_size // exp_local)
    capacity = max(2, 2 * tok_dev * TOP // experts_all)
    flat_ids = expert_ids.reshape(-1)
    onehot = (flat_ids[:, None] == jnp.arange(experts_all, dtype=jnp.int32)[None, :]).astype(
        jnp.int32
    )
    before = jnp.cumsum(onehot, axis=0) - onehot
    slot = flat_ids * capacity + jnp.sum(before * onehot, axis=1)
    slot_match = (
        slot.reshape(tok_dev, TOP)[:, :, None]
        == jnp.arange(experts_all * capacity, dtype=jnp.int32)[None, None, :]
    )
    dispatch_table = jnp.transpose(jnp.any(slot_match, axis=1)).astype(jnp.bfloat16)
    combine_table = jnp.sum(jnp.where(slot_match, gate_weights[:, :, None], 0.0), axis=1)
    buffer = jnp.dot(dispatch_table, expert_in, preferred_element_type=jnp.float32).astype(
        jnp.bfloat16
    )
    buffer = buffer.reshape(tensor_size, exp_local, capacity, width)
    received = lax.all_to_all(buffer, "tensor", split_axis=0, concat_axis=0, tiled=True)
    gate_local = w_gate[0]
    up_local = w_up[0]
    down_local = w_down[0]
    keep_expert = (jnp.arange(exp_local, dtype=jnp.int32) == own_expert)[None, None, :, None, None]
    chosen = lax.dynamic_index_in_dim(
        lax.all_gather(received[None], "seq", axis=0, tiled=True), own_expert, 2, keepdims=False
    )
    gated = jnp.einsum("srcd,df->srcf", chosen, gate_local, preferred_element_type=jnp.float32)
    upward = jnp.einsum("srcd,df->srcf", chosen, up_local, preferred_element_type=jnp.float32)
    activity = (jax.nn.silu(gated) * upward).astype(jnp.bfloat16)
    result = jnp.einsum("srcf,fd->srcd", activity, down_local, preferred_element_type=jnp.float32)
    partials = jnp.where(keep_expert, result[:, :, None], 0.0)
    summed = lax.psum_scatter(
        partials.astype(jnp.bfloat16), "seq", scatter_dimension=0, tiled=True
    ).astype(jnp.float32)
    returned = lax.all_to_all(
        summed[0].astype(jnp.bfloat16), "tensor", split_axis=0, concat_axis=0, tiled=True
    ).astype(jnp.float32)
    moe_sum = jnp.dot(
        combine_table,
        returned.reshape(experts_all * capacity, width),
        preferred_element_type=jnp.float32,
        precision=lax.Precision.HIGHEST,
    )
    output = (mixed_rows.astype(jnp.float32) + moe_sum).astype(jnp.bfloat16)
    return (output, new_keys, new_values)


def solution(mesh):
    return jax.shard_map(
        local,
        mesh=mesh,
        in_specs=(
            P(("seq", "tensor"), None),
            P(),
            P(None, None, "tensor"),
            P("tensor"),
            P("tensor"),
            P("tensor", None),
            P("seq", None, "tensor"),
            P("seq", None, "tensor"),
            P(),
            P(),
            P(),
            P(),
            P(("seq", "tensor"), None),
            P(("seq", "tensor"), None),
            P(("tensor", "seq"), None, None),
            P(("tensor", "seq"), None, None),
            P(("tensor", "seq"), None, None),
        ),
        out_specs=(P(("seq", "tensor"), None), P("seq", "tensor"), P("seq", "tensor")),
        check_vma=False,
    )
```

```python
import jax
import jax.numpy as jnp
from jax import lax
from jax.sharding import PartitionSpec as P

HD = 128
TOP = 8
EXP_DEV = 2


def from_partner(value, axis, stride):
    mask = 2**stride
    pairs = [(source, source ^ mask) for source in range(lax.axis_size(axis))]
    return lax.ppermute(value, axis, pairs)


def passed_along(value, axis, by):
    devices = lax.axis_size(axis)
    pairs = [(i, i + by) for i in range(devices) if 0 <= i + by < devices]
    return lax.ppermute(value, axis, pairs)


def gather_by_exchange(value, axis):
    devices = lax.axis_size(axis)
    copies = jnp.broadcast_to(value[None], (devices,) + value.shape)
    got = lax.all_to_all(copies, axis, 0, 0, tiled=True)
    return got


def rms_scale(values, gain):
    mean_square = jnp.mean(values * values, axis=-1, keepdims=True)
    return values * lax.rsqrt(mean_square + 1e-05) * gain.astype(jnp.float32)


def attend_block(carry, queries_heads, block, mask):
    largest, total, accum = carry
    heads_local = queries_heads.shape[1]
    count = block.shape[0]
    key_block = block[:, 0].reshape(count, heads_local, HD)
    value_block = block[:, 1].reshape(count, heads_local, HD)
    scores = jnp.einsum(
        "qhd,khd->hqk", queries_heads, key_block, preferred_element_type=jnp.float32
    ) * HD ** (-0.5)
    scores = jnp.where(mask[None], scores, -1e30)
    new_largest = jnp.maximum(largest, jnp.max(scores, axis=-1))
    weights = jnp.where(mask[None], jnp.exp(scores - new_largest[:, :, None]), 0.0)
    factor = jnp.exp(largest - new_largest)
    total = total * factor + jnp.sum(weights, axis=-1)
    update = jnp.einsum(
        "hqk,khd->hqd",
        weights.astype(jnp.bfloat16),
        value_block,
        preferred_element_type=jnp.float32,
    )
    accum = accum * factor[:, :, None] + update
    return (new_largest, total, accum)


def local(
    tokens,
    attn_gain,
    w_qkv,
    q_gain,
    k_gain,
    w_out,
    prefix_keys,
    prefix_values,
    segments,
    request_group,
    prefix_owner,
    mlp_gain,
    expert_ids,
    gate_weights,
    w_gate,
    w_up,
    w_down,
):
    tensor_size = lax.axis_size("tensor")
    seq_size = lax.axis_size("seq")
    seq_index = lax.axis_index("seq")
    tensor_index = lax.axis_index("tensor")
    tok_dev = tokens.shape[0]
    width = tokens.shape[1]
    tok_seq = tok_dev * tensor_size
    columns = w_qkv.shape[2]
    lower_bit = tensor_index % 2
    prefix_own = jnp.stack([prefix_keys[0], prefix_values[0]], axis=1)
    prefix_partner = from_partner(prefix_own, "tensor", 0)
    prefix_full = jnp.where(
        lower_bit == 0,
        jnp.concatenate([prefix_own, prefix_partner], axis=-1),
        jnp.concatenate([prefix_partner, prefix_own], axis=-1),
    )
    piece = lax.all_gather(prefix_full[None], "seq", axis=0, tiled=True)
    normed = rms_scale(tokens.astype(jnp.float32), attn_gain).astype(jnp.bfloat16)
    w_flat = w_qkv.reshape(width, 3 * columns)
    projected = jnp.dot(
        gather_by_exchange(normed, "tensor").reshape(tok_seq, width),
        w_flat,
        preferred_element_type=jnp.float32,
    )
    query_part = projected[:, :columns]
    key_part = projected[:, columns : 2 * columns]
    partial_squares = jnp.stack(
        [jnp.sum(query_part * query_part, axis=-1), jnp.sum(key_part * key_part, axis=-1)]
    )
    squares = jnp.sum(gather_by_exchange(partial_squares, "tensor"), axis=0)
    query_rows = (
        query_part * lax.rsqrt(squares[0] / width + 1e-05)[:, None] * q_gain.astype(jnp.float32)
    ).astype(jnp.bfloat16)
    new_keys = (
        key_part * lax.rsqrt(squares[1] / width + 1e-05)[:, None] * k_gain.astype(jnp.float32)
    ).astype(jnp.bfloat16)
    new_values = projected[:, 2 * columns :].astype(jnp.bfloat16)
    stacked = jnp.stack([new_keys, new_values], axis=1)
    half_rows = tok_seq // 2
    partner = from_partner(stacked, "tensor", 0)
    suffix_full = jnp.where(
        lower_bit == 0,
        jnp.concatenate([stacked, partner], axis=-1),
        jnp.concatenate([partner, stacked], axis=-1),
    )
    query_halves = query_rows.reshape(2, half_rows, columns)
    own_half = lax.dynamic_index_in_dim(query_halves, lower_bit, 0, keepdims=False)
    send_half = lax.dynamic_index_in_dim(query_halves, 1 - lower_bit, 0, keepdims=False)
    got_half = from_partner(send_half, "tensor", 0)
    query_full = jnp.where(
        lower_bit == 0,
        jnp.concatenate([own_half, got_half], axis=-1),
        jnp.concatenate([got_half, own_half], axis=-1),
    )
    query_offset = lower_bit * half_rows
    heads_local = 1
    queries_heads = query_full.reshape(half_rows, heads_local, HD)
    groups_count = prefix_owner.shape[0]
    request_count = request_group.shape[0]
    token_group = jnp.sum(
        jnp.where(
            segments[:, None] == jnp.arange(request_count, dtype=jnp.int32)[None, :],
            request_group[None, :],
            0,
        ),
        axis=1,
    )
    base_row = seq_index * tok_seq
    query_start = base_row + query_offset
    query_seg = lax.dynamic_slice_in_dim(segments, query_start, half_rows, 0)
    query_group = lax.dynamic_slice_in_dim(token_group, query_start, half_rows, 0)
    query_pos = query_start + jnp.arange(half_rows, dtype=jnp.int32)
    padded_seg = jnp.concatenate([jnp.full((tok_seq,), -1, jnp.int32), segments], axis=0)
    key_seg = lax.dynamic_slice_in_dim(padded_seg, base_row, 2 * tok_seq, 0)
    key_pos = base_row - tok_seq + jnp.arange(2 * tok_seq, dtype=jnp.int32)
    previous = passed_along(suffix_full, "seq", 1)
    suffix_keys = jnp.concatenate([previous, suffix_full], axis=0)
    suffix_mask = (key_seg[None, :] == query_seg[:, None]) & (
        key_pos[None, :] <= query_pos[:, None]
    )
    carry = (
        jnp.full((heads_local, half_rows), -1e30, jnp.float32),
        jnp.zeros((heads_local, half_rows), jnp.float32),
        jnp.zeros((heads_local, half_rows, HD), jnp.float32),
    )
    carry = attend_block(carry, queries_heads, suffix_keys, suffix_mask)
    owner_of_query = jnp.sum(
        jnp.where(
            query_group[:, None] == jnp.arange(groups_count, dtype=jnp.int32)[None, :],
            prefix_owner[None, :],
            0,
        ),
        axis=1,
    )
    state = carry
    start = jnp.int32(0)
    for offset in range(piece.shape[0]):
        slot_mask = (owner_of_query == start + offset)[:, None]
        state = attend_block(state, queries_heads, piece[offset], slot_mask)
    carry = state
    attended = (carry[2] / carry[1][:, :, None]).astype(jnp.bfloat16)
    attended = jnp.transpose(attended, (1, 0, 2)).reshape(half_rows, heads_local * HD)
    split_out = attended.reshape(half_rows, 2, columns)
    own_out = lax.dynamic_index_in_dim(split_out, lower_bit, 1, keepdims=False)
    send_out = lax.dynamic_index_in_dim(split_out, 1 - lower_bit, 1, keepdims=False)
    got_out = from_partner(send_out, "tensor", 0)
    attended_local = jnp.where(
        lower_bit == 0,
        jnp.concatenate([own_out, got_out], axis=0),
        jnp.concatenate([got_out, own_out], axis=0),
    )
    attn_partial = jnp.dot(attended_local, w_out, preferred_element_type=jnp.float32)
    attn_partial = attn_partial.astype(jnp.bfloat16).reshape(tensor_size, tok_dev, width)
    attn_sum = jnp.sum(
        lax.all_to_all(attn_partial, "tensor", 0, 0, tiled=True).astype(jnp.float32), axis=0
    )
    mixed_rows = (tokens.astype(jnp.float32) + attn_sum).astype(jnp.bfloat16)
    expert_in = rms_scale(mixed_rows.astype(jnp.float32), mlp_gain).astype(jnp.bfloat16)
    exp_local = EXP_DEV
    experts_all = exp_local * tensor_size
    own_expert = seq_index // (seq_size // exp_local)
    capacity = max(2, 2 * tok_dev * TOP // experts_all)
    flat_ids = expert_ids.reshape(-1)
    onehot = (flat_ids[:, None] == jnp.arange(experts_all, dtype=jnp.int32)[None, :]).astype(
        jnp.int32
    )
    before = jnp.cumsum(onehot, axis=0) - onehot
    slot = flat_ids * capacity + jnp.sum(before * onehot, axis=1)
    slot_match = (
        slot.reshape(tok_dev, TOP)[:, :, None]
        == jnp.arange(experts_all * capacity, dtype=jnp.int32)[None, None, :]
    )
    dispatch_table = jnp.transpose(jnp.any(slot_match, axis=1)).astype(jnp.bfloat16)
    combine_table = jnp.sum(jnp.where(slot_match, gate_weights[:, :, None], 0.0), axis=1)
    buffer = jnp.dot(dispatch_table, expert_in, preferred_element_type=jnp.float32).astype(
        jnp.bfloat16
    )
    buffer = buffer.reshape(tensor_size, exp_local, capacity, width)
    received = lax.all_to_all(buffer, "tensor", split_axis=0, concat_axis=0, tiled=True)
    gate_local = w_gate[0]
    up_local = w_up[0]
    down_local = w_down[0]
    holders = seq_size // exp_local
    per_expert = jnp.transpose(received, (1, 0, 2, 3))
    chosen = lax.all_to_all(jnp.repeat(per_expert, holders, axis=0), "seq", 0, 0, tiled=True)
    gated = jnp.einsum("srcd,df->srcf", chosen, gate_local, preferred_element_type=jnp.float32)
    upward = jnp.einsum("srcd,df->srcf", chosen, up_local, preferred_element_type=jnp.float32)
    activity = (jax.nn.silu(gated) * upward).astype(jnp.bfloat16)
    result = jnp.einsum("srcf,fd->srcd", activity, down_local, preferred_element_type=jnp.float32)
    back = lax.all_to_all(result.astype(jnp.bfloat16), "seq", 0, 0, tiled=True)
    summed = jnp.sum(
        back.astype(jnp.float32).reshape((exp_local, holders) + back.shape[1:]), axis=1
    )
    summed = jnp.transpose(summed, (1, 0, 2, 3))
    returned = lax.all_to_all(
        summed.astype(jnp.bfloat16), "tensor", split_axis=0, concat_axis=0, tiled=True
    ).astype(jnp.float32)
    moe_sum = jnp.dot(
        combine_table,
        returned.reshape(experts_all * capacity, width),
        preferred_element_type=jnp.float32,
        precision=lax.Precision.HIGHEST,
    )
    output = (mixed_rows.astype(jnp.float32) + moe_sum).astype(jnp.bfloat16)
    return (output, new_keys, new_values)


def solution(mesh):
    return jax.shard_map(
        local,
        mesh=mesh,
        in_specs=(
            P(("seq", "tensor"), None),
            P(),
            P(None, None, "tensor"),
            P("tensor"),
            P("tensor"),
            P("tensor", None),
            P("seq", None, "tensor"),
            P("seq", None, "tensor"),
            P(),
            P(),
            P(),
            P(),
            P(("seq", "tensor"), None),
            P(("seq", "tensor"), None),
            P(("tensor", "seq"), None, None),
            P(("tensor", "seq"), None, None),
            P(("tensor", "seq"), None, None),
        ),
        out_specs=(P(("seq", "tensor"), None), P("seq", "tensor"), P("seq", "tensor")),
        check_vma=False,
    )
```

```python
import jax
import jax.numpy as jnp
from jax import lax
from jax.sharding import Mesh
from jax.sharding import PartitionSpec as P

HD = 128
TOP = 8
EXP_DEV = 2
HEADS_AXES = ("tz", "tyh")
TENSOR = ("tz", "tyh", "tyl")


def passed_along(value, axis, by):
    devices = lax.axis_size(axis)
    pairs = [(i, i + by) for i in range(devices) if 0 <= i + by < devices]
    return lax.ppermute(value, axis, pairs)


def from_partner(value):
    return lax.ppermute(value, "tyl", [(0, 1), (1, 0)])


def gather_by_exchange(value, axis):
    devices = lax.axis_size(axis)
    copies = jnp.broadcast_to(value[None], (devices,) + value.shape)
    return lax.all_to_all(copies, axis, 0, 0, tiled=True)


def rms_scale(values, gain):
    mean_square = jnp.mean(values * values, axis=-1, keepdims=True)
    return values * lax.rsqrt(mean_square + 1e-05) * gain.astype(jnp.float32)


def attend_block(carry, queries_heads, block, mask):
    largest, total, accum = carry
    heads_local = queries_heads.shape[1]
    count = block.shape[0]
    key_block = block[:, 0].reshape(count, heads_local, HD)
    value_block = block[:, 1].reshape(count, heads_local, HD)
    scores = jnp.einsum(
        "qhd,khd->hqk", queries_heads, key_block, preferred_element_type=jnp.float32
    ) * HD ** (-0.5)
    scores = jnp.where(mask[None], scores, -1e30)
    new_largest = jnp.maximum(largest, jnp.max(scores, axis=-1))
    weights = jnp.where(mask[None], jnp.exp(scores - new_largest[:, :, None]), 0.0)
    factor = jnp.exp(largest - new_largest)
    total = total * factor + jnp.sum(weights, axis=-1)
    update = jnp.einsum(
        "hqk,khd->hqd",
        weights.astype(jnp.bfloat16),
        value_block,
        preferred_element_type=jnp.float32,
    )
    accum = accum * factor[:, :, None] + update
    return (new_largest, total, accum)


def local(
    tokens,
    attn_gain,
    w_qkv,
    q_gain,
    k_gain,
    w_out,
    prefix_keys,
    prefix_values,
    segments,
    request_group,
    prefix_owner,
    mlp_gain,
    expert_ids,
    gate_weights,
    w_gate,
    w_up,
    w_down,
):
    tensor_size = lax.axis_size(TENSOR)
    heads_count = lax.axis_size(HEADS_AXES)
    seq_size = lax.axis_size("seq")
    seq_index = lax.axis_index("seq")
    parity = lax.axis_index("tyl")
    tok_dev = tokens.shape[0]
    width = tokens.shape[1]
    tok_seq = tok_dev * tensor_size
    columns = w_qkv.shape[2]
    rows_half = tok_dev * heads_count

    def join(own, other, axis):
        return jnp.where(
            parity == 0,
            jnp.concatenate([own, other], axis=axis),
            jnp.concatenate([other, own], axis=axis),
        )

    prefix_own = jnp.stack([prefix_keys[0], prefix_values[0]], axis=1)
    piece = lax.all_gather(prefix_own[None], ("seq", "tyl"), axis=0, tiled=True)
    piece = piece.reshape((seq_size, 2) + prefix_own.shape)
    piece = jnp.transpose(piece, (0, 2, 3, 1, 4)).reshape(
        (seq_size,) + prefix_own.shape[:2] + (2 * columns,)
    )
    w_head = join(w_qkv, from_partner(w_qkv), 2)
    out_head = join(w_out, from_partner(w_out), 0)
    gain_pair = jnp.stack([q_gain, k_gain])
    gains = join(gain_pair, from_partner(gain_pair), 1).astype(jnp.float32)

    normed = rms_scale(tokens.astype(jnp.float32), attn_gain).astype(jnp.bfloat16)
    rows = gather_by_exchange(normed, HEADS_AXES).reshape(rows_half, width)
    projected = jnp.dot(
        rows, w_head.reshape(width, 3 * 2 * columns), preferred_element_type=jnp.float32
    ).reshape(rows_half, 3, 2 * columns)
    query_part = projected[:, 0]
    key_part = projected[:, 1]
    partial_squares = jnp.stack(
        [jnp.sum(query_part * query_part, axis=-1), jnp.sum(key_part * key_part, axis=-1)]
    )
    squares = jnp.sum(gather_by_exchange(partial_squares, HEADS_AXES), axis=0)
    queries = (
        query_part * lax.rsqrt(squares[0] / width + 1e-05)[:, None] * gains[0]
    ).astype(jnp.bfloat16)
    keys = (key_part * lax.rsqrt(squares[1] / width + 1e-05)[:, None] * gains[1]).astype(
        jnp.bfloat16
    )
    values = projected[:, 2].astype(jnp.bfloat16)
    own_kv = jnp.stack([keys, values], axis=1)
    other_kv = from_partner(own_kv)
    kv_shape = (heads_count, 1, tok_dev, 2, 2 * columns)
    suffix_full = join(own_kv.reshape(kv_shape), other_kv.reshape(kv_shape), 1).reshape(
        tok_seq, 2, 2 * columns
    )
    own_cols = jnp.where(parity == 0, suffix_full[..., :columns], suffix_full[..., columns:])
    new_keys = own_cols[:, 0]
    new_values = own_cols[:, 1]

    groups_count = prefix_owner.shape[0]
    request_count = request_group.shape[0]
    token_group = jnp.sum(
        jnp.where(
            segments[:, None] == jnp.arange(request_count, dtype=jnp.int32)[None, :],
            request_group[None, :],
            0,
        ),
        axis=1,
    )
    base_row = seq_index * tok_seq
    seq_segments = lax.dynamic_slice_in_dim(segments, base_row, tok_seq, 0)
    seq_groups = lax.dynamic_slice_in_dim(token_group, base_row, tok_seq, 0)

    def own_rows(values_of_seq):
        halves = values_of_seq.reshape(heads_count, 2, tok_dev)
        return jnp.where(parity == 0, halves[:, 0], halves[:, 1]).reshape(rows_half)

    query_seg = own_rows(seq_segments)
    query_group = own_rows(seq_groups)
    query_pos = own_rows(base_row + jnp.arange(tok_seq, dtype=jnp.int32))
    padded_seg = jnp.concatenate([jnp.full((tok_seq,), -1, jnp.int32), segments], axis=0)
    key_seg = lax.dynamic_slice_in_dim(padded_seg, base_row, 2 * tok_seq, 0)
    key_pos = base_row - tok_seq + jnp.arange(2 * tok_seq, dtype=jnp.int32)
    previous = passed_along(suffix_full, "seq", 1)
    suffix_keys = jnp.concatenate([previous, suffix_full], axis=0)
    suffix_mask = (key_seg[None, :] == query_seg[:, None]) & (
        key_pos[None, :] <= query_pos[:, None]
    )
    heads_local = 1
    queries_heads = queries.reshape(rows_half, heads_local, HD)
    carry = (
        jnp.full((heads_local, rows_half), -1e30, jnp.float32),
        jnp.zeros((heads_local, rows_half), jnp.float32),
        jnp.zeros((heads_local, rows_half, HD), jnp.float32),
    )
    carry = attend_block(carry, queries_heads, suffix_keys, suffix_mask)
    owner_of_query = jnp.sum(
        jnp.where(
            query_group[:, None] == jnp.arange(groups_count, dtype=jnp.int32)[None, :],
            prefix_owner[None, :],
            0,
        ),
        axis=1,
    )
    for slot in range(seq_size):
        slot_mask = (owner_of_query == slot)[:, None]
        carry = attend_block(carry, queries_heads, piece[slot], slot_mask)
    attended = (carry[2] / carry[1][:, :, None]).astype(jnp.bfloat16)
    attended = jnp.transpose(attended, (1, 0, 2)).reshape(rows_half, heads_local * HD)
    attn_partial = jnp.dot(attended, out_head, preferred_element_type=jnp.float32)
    attn_partial = attn_partial.astype(jnp.bfloat16).reshape(heads_count, tok_dev, width)
    attn_sum = jnp.sum(
        lax.all_to_all(attn_partial, HEADS_AXES, 0, 0, tiled=True).astype(jnp.float32), axis=0
    )
    mixed_rows = (tokens.astype(jnp.float32) + attn_sum).astype(jnp.bfloat16)
    expert_in = rms_scale(mixed_rows.astype(jnp.float32), mlp_gain).astype(jnp.bfloat16)
    exp_local = EXP_DEV
    experts_all = exp_local * tensor_size
    own_expert = seq_index // (seq_size // exp_local)
    capacity = max(2, 2 * tok_dev * TOP // experts_all)
    flat_ids = expert_ids.reshape(-1)
    onehot = (flat_ids[:, None] == jnp.arange(experts_all, dtype=jnp.int32)[None, :]).astype(
        jnp.int32
    )
    before = jnp.cumsum(onehot, axis=0) - onehot
    slot = flat_ids * capacity + jnp.sum(before * onehot, axis=1)
    slot_match = (
        slot.reshape(tok_dev, TOP)[:, :, None]
        == jnp.arange(experts_all * capacity, dtype=jnp.int32)[None, None, :]
    )
    dispatch_table = jnp.transpose(jnp.any(slot_match, axis=1)).astype(jnp.bfloat16)
    combine_table = jnp.sum(jnp.where(slot_match, gate_weights[:, :, None], 0.0), axis=1)
    buffer = jnp.dot(dispatch_table, expert_in, preferred_element_type=jnp.float32).astype(
        jnp.bfloat16
    )
    buffer = buffer.reshape(tensor_size, exp_local, capacity, width)
    received = lax.all_to_all(buffer, TENSOR, split_axis=0, concat_axis=0, tiled=True)
    gate_local = w_gate[0]
    up_local = w_up[0]
    down_local = w_down[0]
    holders = seq_size // exp_local
    per_expert = jnp.transpose(received, (1, 0, 2, 3))
    chosen = lax.all_to_all(jnp.repeat(per_expert, holders, axis=0), "seq", 0, 0, tiled=True)
    gated = jnp.einsum("srcd,df->srcf", chosen, gate_local, preferred_element_type=jnp.float32)
    upward = jnp.einsum("srcd,df->srcf", chosen, up_local, preferred_element_type=jnp.float32)
    activity = (jax.nn.silu(gated) * upward).astype(jnp.bfloat16)
    result = jnp.einsum("srcf,fd->srcd", activity, down_local, preferred_element_type=jnp.float32)
    back = lax.all_to_all(result.astype(jnp.bfloat16), "seq", 0, 0, tiled=True)
    summed = jnp.sum(
        back.astype(jnp.float32).reshape((exp_local, holders) + back.shape[1:]), axis=1
    )
    summed = jnp.transpose(summed, (1, 0, 2, 3))
    returned = lax.all_to_all(
        summed.astype(jnp.bfloat16), TENSOR, split_axis=0, concat_axis=0, tiled=True
    ).astype(jnp.float32)
    moe_sum = jnp.dot(
        combine_table,
        returned.reshape(experts_all * capacity, width),
        preferred_element_type=jnp.float32,
        precision=lax.Precision.HIGHEST,
    )
    output = (mixed_rows.astype(jnp.float32) + moe_sum).astype(jnp.bfloat16)
    return (output, new_keys, new_values)


def solution(mesh):
    seq_size, tensor_size = mesh.devices.shape
    tz = tensor_size // 4
    grid = Mesh(mesh.devices.reshape(seq_size, tz, 2, 2), ("seq",) + TENSOR)
    rows = ("seq",) + TENSOR
    return jax.shard_map(
        local,
        mesh=grid,
        in_specs=(
            P(rows, None),
            P(),
            P(None, None, TENSOR),
            P(TENSOR),
            P(TENSOR),
            P(TENSOR, None),
            P("seq", None, TENSOR),
            P("seq", None, TENSOR),
            P(),
            P(),
            P(),
            P(),
            P(rows, None),
            P(rows, None),
            P(TENSOR + ("seq",), None, None),
            P(TENSOR + ("seq",), None, None),
            P(TENSOR + ("seq",), None, None),
        ),
        out_specs=(P(rows, None), P("seq", TENSOR), P("seq", TENSOR)),
        check_vma=False,
    )
```

```python
import jax
import jax.numpy as jnp
from jax import lax
from jax.sharding import PartitionSpec as P

HD = 128
TOP = 8
EXP_DEV = 2


def from_partner(value, axis, stride):
    mask = 2**stride
    pairs = [(source, source ^ mask) for source in range(lax.axis_size(axis))]
    return lax.ppermute(value, axis, pairs)


def passed_along(value, axis, by):
    devices = lax.axis_size(axis)
    pairs = [(i, i + by) for i in range(devices) if 0 <= i + by < devices]
    return lax.ppermute(value, axis, pairs)


def gather_by_exchange(value, axis):
    devices = lax.axis_size(axis)
    copies = jnp.broadcast_to(value[None], (devices,) + value.shape)
    got = lax.all_to_all(copies, axis, 0, 0, tiled=True)
    return got


def rms_scale(values, gain):
    mean_square = jnp.mean(values * values, axis=-1, keepdims=True)
    return values * lax.rsqrt(mean_square + 1e-05) * gain.astype(jnp.float32)


def attend_block(carry, queries_heads, block, mask):
    largest, total, accum = carry
    heads_local = queries_heads.shape[1]
    count = block.shape[0]
    key_block = block[:, 0].reshape(count, heads_local, HD)
    value_block = block[:, 1].reshape(count, heads_local, HD)
    scores = jnp.einsum(
        "qhd,khd->hqk", queries_heads, key_block, preferred_element_type=jnp.float32
    ) * HD ** (-0.5)
    scores = jnp.where(mask[None], scores, -1e30)
    new_largest = jnp.maximum(largest, jnp.max(scores, axis=-1))
    weights = jnp.where(mask[None], jnp.exp(scores - new_largest[:, :, None]), 0.0)
    factor = jnp.exp(largest - new_largest)
    total = total * factor + jnp.sum(weights, axis=-1)
    update = jnp.einsum(
        "hqk,khd->hqd",
        weights.astype(jnp.bfloat16),
        value_block,
        preferred_element_type=jnp.float32,
    )
    accum = accum * factor[:, :, None] + update
    return (new_largest, total, accum)


def local(
    tokens,
    attn_gain,
    w_qkv,
    q_gain,
    k_gain,
    w_out,
    prefix_keys,
    prefix_values,
    segments,
    request_group,
    prefix_owner,
    mlp_gain,
    expert_ids,
    gate_weights,
    w_gate,
    w_up,
    w_down,
):
    tensor_size = lax.axis_size("tensor")
    seq_size = lax.axis_size("seq")
    seq_index = lax.axis_index("seq")
    tensor_index = lax.axis_index("tensor")
    tok_dev = tokens.shape[0]
    width = tokens.shape[1]
    tok_seq = tok_dev * tensor_size
    columns = w_qkv.shape[2]
    lower_bit = tensor_index % 2
    prefix_own = jnp.stack([prefix_keys[0], prefix_values[0]], axis=1)
    prefix_partner = from_partner(prefix_own, "tensor", 0)
    prefix_full = jnp.where(
        lower_bit == 0,
        jnp.concatenate([prefix_own, prefix_partner], axis=-1),
        jnp.concatenate([prefix_partner, prefix_own], axis=-1),
    )
    piece = lax.all_gather(prefix_full[None], "seq", axis=0, tiled=True)
    gains_in = from_partner(jnp.stack([q_gain, k_gain]), "tensor", 0)
    normed = rms_scale(tokens.astype(jnp.float32), attn_gain).astype(jnp.bfloat16)
    w_flat = w_qkv.reshape(width, 3 * columns)
    rows = gather_by_exchange(normed, "tensor").reshape(tok_seq, width)
    projected = jnp.dot(
        rows,
        w_flat,
        preferred_element_type=jnp.float32,
    )
    query_part = projected[:, :columns]
    key_part = projected[:, columns : 2 * columns]
    value_part = projected[:, 2 * columns :]
    partial_squares = jnp.stack(
        [jnp.sum(query_part * query_part, axis=-1), jnp.sum(key_part * key_part, axis=-1)]
    )
    half_rows = tok_seq // 2
    query_halves = query_part.reshape(2, half_rows, columns)
    own_half = lax.dynamic_index_in_dim(query_halves, lower_bit, 0, keepdims=False)
    send_half = lax.dynamic_index_in_dim(query_halves, 1 - lower_bit, 0, keepdims=False)
    raw_out = jnp.concatenate([send_half, key_part, value_part], axis=0)
    raw_out, partial_squares = lax.optimization_barrier((raw_out, partial_squares))
    raw_in = from_partner(raw_out, "tensor", 0)
    got_half = raw_in[:half_rows]
    got_keys = raw_in[half_rows : half_rows + tok_seq]
    got_values = raw_in[half_rows + tok_seq :]
    squares = jnp.sum(gather_by_exchange(partial_squares, "tensor"), axis=0)
    query_scale = lax.rsqrt(squares[0] / width + 1e-05)[:, None]
    key_scale = lax.rsqrt(squares[1] / width + 1e-05)[:, None]
    own_scale = lax.dynamic_index_in_dim(
        query_scale.reshape(2, half_rows, 1), lower_bit, 0, keepdims=False
    )
    own_query = (own_half * own_scale * q_gain.astype(jnp.float32)).astype(jnp.bfloat16)
    got_query = (got_half * own_scale * gains_in[0].astype(jnp.float32)).astype(jnp.bfloat16)
    new_keys = (key_part * key_scale * k_gain.astype(jnp.float32)).astype(jnp.bfloat16)
    new_values = value_part.astype(jnp.bfloat16)
    partner_keys = (got_keys * key_scale * gains_in[1].astype(jnp.float32)).astype(jnp.bfloat16)
    stacked = jnp.stack([new_keys, new_values], axis=1)
    partner = jnp.stack([partner_keys, got_values.astype(jnp.bfloat16)], axis=1)
    suffix_full = jnp.where(
        lower_bit == 0,
        jnp.concatenate([stacked, partner], axis=-1),
        jnp.concatenate([partner, stacked], axis=-1),
    )
    query_full = jnp.where(
        lower_bit == 0,
        jnp.concatenate([own_query, got_query], axis=-1),
        jnp.concatenate([got_query, own_query], axis=-1),
    )
    query_offset = lower_bit * half_rows
    heads_local = 1
    queries_heads = query_full.reshape(half_rows, heads_local, HD)
    groups_count = prefix_owner.shape[0]
    request_count = request_group.shape[0]
    token_group = jnp.sum(
        jnp.where(
            segments[:, None] == jnp.arange(request_count, dtype=jnp.int32)[None, :],
            request_group[None, :],
            0,
        ),
        axis=1,
    )
    base_row = seq_index * tok_seq
    query_start = base_row + query_offset
    query_seg = lax.dynamic_slice_in_dim(segments, query_start, half_rows, 0)
    query_group = lax.dynamic_slice_in_dim(token_group, query_start, half_rows, 0)
    query_pos = query_start + jnp.arange(half_rows, dtype=jnp.int32)
    padded_seg = jnp.concatenate([jnp.full((tok_seq,), -1, jnp.int32), segments], axis=0)
    key_seg = lax.dynamic_slice_in_dim(padded_seg, base_row, 2 * tok_seq, 0)
    key_pos = base_row - tok_seq + jnp.arange(2 * tok_seq, dtype=jnp.int32)
    previous = passed_along(suffix_full, "seq", 1)
    suffix_keys = jnp.concatenate([previous, suffix_full], axis=0)
    suffix_mask = (key_seg[None, :] == query_seg[:, None]) & (
        key_pos[None, :] <= query_pos[:, None]
    )
    carry = (
        jnp.full((heads_local, half_rows), -1e30, jnp.float32),
        jnp.zeros((heads_local, half_rows), jnp.float32),
        jnp.zeros((heads_local, half_rows, HD), jnp.float32),
    )
    carry = attend_block(carry, queries_heads, suffix_keys, suffix_mask)
    owner_of_query = jnp.sum(
        jnp.where(
            query_group[:, None] == jnp.arange(groups_count, dtype=jnp.int32)[None, :],
            prefix_owner[None, :],
            0,
        ),
        axis=1,
    )
    state = carry
    start = jnp.int32(0)
    for offset in range(piece.shape[0]):
        slot_mask = (owner_of_query == start + offset)[:, None]
        state = attend_block(state, queries_heads, piece[offset], slot_mask)
    carry = state
    attended = (carry[2] / carry[1][:, :, None]).astype(jnp.bfloat16)
    attended = jnp.transpose(attended, (1, 0, 2)).reshape(half_rows, heads_local * HD)
    split_out = attended.reshape(half_rows, 2, columns)
    own_out = lax.dynamic_index_in_dim(split_out, lower_bit, 1, keepdims=False)
    send_out = lax.dynamic_index_in_dim(split_out, 1 - lower_bit, 1, keepdims=False)
    got_out = from_partner(send_out, "tensor", 0)
    attended_local = jnp.where(
        lower_bit == 0,
        jnp.concatenate([own_out, got_out], axis=0),
        jnp.concatenate([got_out, own_out], axis=0),
    )
    attn_partial = jnp.dot(attended_local, w_out, preferred_element_type=jnp.float32)
    attn_partial = attn_partial.astype(jnp.bfloat16).reshape(tensor_size, tok_dev, width)
    attn_sum = jnp.sum(
        lax.all_to_all(attn_partial, "tensor", 0, 0, tiled=True).astype(jnp.float32), axis=0
    )
    mixed_rows = (tokens.astype(jnp.float32) + attn_sum).astype(jnp.bfloat16)
    expert_in = rms_scale(mixed_rows.astype(jnp.float32), mlp_gain).astype(jnp.bfloat16)
    exp_local = EXP_DEV
    experts_all = exp_local * tensor_size
    capacity = max(2, 2 * tok_dev * TOP // experts_all)
    flat_ids = expert_ids.reshape(-1)
    onehot = (flat_ids[:, None] == jnp.arange(experts_all, dtype=jnp.int32)[None, :]).astype(
        jnp.int32
    )
    before = jnp.cumsum(onehot, axis=0) - onehot
    slot = flat_ids * capacity + jnp.sum(before * onehot, axis=1)
    slot_match = (
        slot.reshape(tok_dev, TOP)[:, :, None]
        == jnp.arange(experts_all * capacity, dtype=jnp.int32)[None, None, :]
    )
    dispatch_table = jnp.transpose(jnp.any(slot_match, axis=1)).astype(jnp.bfloat16)
    combine_table = jnp.sum(jnp.where(slot_match, gate_weights[:, :, None], 0.0), axis=1)
    buffer = jnp.dot(dispatch_table, expert_in, preferred_element_type=jnp.float32).astype(
        jnp.bfloat16
    )
    buffer = buffer.reshape(tensor_size, exp_local, capacity, width)
    received = lax.all_to_all(buffer, "tensor", split_axis=0, concat_axis=0, tiled=True)
    gate_local = w_gate[0]
    up_local = w_up[0]
    down_local = w_down[0]
    holders = seq_size // exp_local
    per_expert = jnp.transpose(received, (1, 0, 2, 3))
    chosen = lax.all_to_all(jnp.repeat(per_expert, holders, axis=0), "seq", 0, 0, tiled=True)
    gated = jnp.einsum("srcd,df->srcf", chosen, gate_local, preferred_element_type=jnp.float32)
    upward = jnp.einsum("srcd,df->srcf", chosen, up_local, preferred_element_type=jnp.float32)
    activity = (jax.nn.silu(gated) * upward).astype(jnp.bfloat16)
    result = jnp.einsum("srcf,fd->srcd", activity, down_local, preferred_element_type=jnp.float32)
    back = lax.all_to_all(result.astype(jnp.bfloat16), "seq", 0, 0, tiled=True)
    summed = jnp.sum(
        back.astype(jnp.float32).reshape((exp_local, holders) + back.shape[1:]), axis=1
    )
    summed = jnp.transpose(summed, (1, 0, 2, 3))
    returned = lax.all_to_all(
        summed.astype(jnp.bfloat16), "tensor", split_axis=0, concat_axis=0, tiled=True
    ).astype(jnp.float32)
    moe_sum = jnp.dot(
        combine_table,
        returned.reshape(experts_all * capacity, width),
        preferred_element_type=jnp.float32,
        precision=lax.Precision.HIGHEST,
    )
    output = (mixed_rows.astype(jnp.float32) + moe_sum).astype(jnp.bfloat16)
    return (output, new_keys, new_values)


def solution(mesh):
    return jax.shard_map(
        local,
        mesh=mesh,
        in_specs=(
            P(("seq", "tensor"), None),
            P(),
            P(None, None, "tensor"),
            P("tensor"),
            P("tensor"),
            P("tensor", None),
            P("seq", None, "tensor"),
            P("seq", None, "tensor"),
            P(),
            P(),
            P(),
            P(),
            P(("seq", "tensor"), None),
            P(("seq", "tensor"), None),
            P(("tensor", "seq"), None, None),
            P(("tensor", "seq"), None, None),
            P(("tensor", "seq"), None, None),
        ),
        out_specs=(P(("seq", "tensor"), None), P("seq", "tensor"), P("seq", "tensor")),
        check_vma=False,
    )
```

```python
import jax
import jax.numpy as jnp
from jax import lax
from jax.sharding import Mesh
from jax.sharding import PartitionSpec as P

HD = 128
TOP = 8
EXP_DEV = 2
TENSOR = ("th", "tyl")


def from_partner(value):
    return lax.ppermute(value, "tyl", [(0, 1), (1, 0)])


def passed_along(value, axis, by):
    devices = lax.axis_size(axis)
    pairs = [(i, i + by) for i in range(devices) if 0 <= i + by < devices]
    return lax.ppermute(value, axis, pairs)


def gather_by_exchange(value, axis):
    devices = lax.axis_size(axis)
    copies = jnp.broadcast_to(value[None], (devices,) + value.shape)
    got = lax.all_to_all(copies, axis, 0, 0, tiled=True)
    return got


def rms_scale(values, gain):
    mean_square = jnp.mean(values * values, axis=-1, keepdims=True)
    return values * lax.rsqrt(mean_square + 1e-05) * gain.astype(jnp.float32)


def attend_block(carry, queries_heads, block, mask):
    largest, total, accum = carry
    heads_local = queries_heads.shape[1]
    count = block.shape[0]
    key_block = block[:, 0].reshape(count, heads_local, HD)
    value_block = block[:, 1].reshape(count, heads_local, HD)
    scores = jnp.einsum(
        "qhd,khd->hqk", queries_heads, key_block, preferred_element_type=jnp.float32
    ) * HD ** (-0.5)
    scores = jnp.where(mask[None], scores, -1e30)
    new_largest = jnp.maximum(largest, jnp.max(scores, axis=-1))
    weights = jnp.where(mask[None], jnp.exp(scores - new_largest[:, :, None]), 0.0)
    factor = jnp.exp(largest - new_largest)
    total = total * factor + jnp.sum(weights, axis=-1)
    update = jnp.einsum(
        "hqk,khd->hqd",
        weights.astype(jnp.bfloat16),
        value_block,
        preferred_element_type=jnp.float32,
    )
    accum = accum * factor[:, :, None] + update
    return (new_largest, total, accum)


def attend_halves(carry, queries_heads, halves, mask):
    largest, total, accum = carry
    rows = queries_heads.shape[0]
    split_queries = queries_heads.reshape(rows, 2, HD // 2)
    scores = jnp.einsum(
        "qcd,ckd->qk", split_queries, halves[:, :, 0], preferred_element_type=jnp.float32
    )[None] * HD ** (-0.5)
    scores = jnp.where(mask[None], scores, -1e30)
    new_largest = jnp.maximum(largest, jnp.max(scores, axis=-1))
    weights = jnp.where(mask[None], jnp.exp(scores - new_largest[:, :, None]), 0.0)
    factor = jnp.exp(largest - new_largest)
    total = total * factor + jnp.sum(weights, axis=-1)
    update = jnp.einsum(
        "qk,ckd->qcd",
        weights[0].astype(jnp.bfloat16),
        halves[:, :, 1],
        preferred_element_type=jnp.float32,
    ).reshape(1, rows, HD)
    accum = accum * factor[:, :, None] + update
    return (new_largest, total, accum)


def local(
    tokens,
    attn_gain,
    w_qkv,
    q_gain,
    k_gain,
    w_out,
    prefix_keys,
    prefix_values,
    segments,
    request_group,
    prefix_owner,
    mlp_gain,
    expert_ids,
    gate_weights,
    w_gate,
    w_up,
    w_down,
):
    tensor_size = lax.axis_size(TENSOR)
    seq_size = lax.axis_size("seq")
    seq_index = lax.axis_index("seq")
    tensor_index = lax.axis_index(TENSOR)
    tok_dev = tokens.shape[0]
    width = tokens.shape[1]
    tok_seq = tok_dev * tensor_size
    columns = w_qkv.shape[2]
    lower_bit = tensor_index % 2
    prefix_own = jnp.stack([prefix_keys[0], prefix_values[0]], axis=1)
    piece = lax.all_gather(prefix_own[None], ("seq", "tyl"), axis=0, tiled=True)
    gains_in = from_partner(jnp.stack([q_gain, k_gain]))
    normed = rms_scale(tokens.astype(jnp.float32), attn_gain).astype(jnp.bfloat16)
    w_flat = w_qkv.reshape(width, 3 * columns)
    rows = gather_by_exchange(normed, TENSOR).reshape(tok_seq, width)
    projected = jnp.dot(
        rows,
        w_flat,
        preferred_element_type=jnp.float32,
    )
    query_part = projected[:, :columns]
    key_part = projected[:, columns : 2 * columns]
    value_part = projected[:, 2 * columns :]
    partial_squares = jnp.stack(
        [jnp.sum(query_part * query_part, axis=-1), jnp.sum(key_part * key_part, axis=-1)]
    )
    half_rows = tok_seq // 2
    query_halves = query_part.reshape(2, half_rows, columns)
    own_half = lax.dynamic_index_in_dim(query_halves, lower_bit, 0, keepdims=False)
    send_half = lax.dynamic_index_in_dim(query_halves, 1 - lower_bit, 0, keepdims=False)
    raw_out = jnp.concatenate([send_half, key_part, value_part], axis=0)
    raw_out, partial_squares = lax.optimization_barrier((raw_out, partial_squares))
    raw_in = from_partner(raw_out)
    got_half = raw_in[:half_rows]
    got_keys = raw_in[half_rows : half_rows + tok_seq]
    got_values = raw_in[half_rows + tok_seq :]
    squares = jnp.sum(gather_by_exchange(partial_squares, TENSOR), axis=0)
    query_scale = lax.rsqrt(squares[0] / width + 1e-05)[:, None]
    key_scale = lax.rsqrt(squares[1] / width + 1e-05)[:, None]
    own_scale = lax.dynamic_index_in_dim(
        query_scale.reshape(2, half_rows, 1), lower_bit, 0, keepdims=False
    )
    own_query = (own_half * own_scale * q_gain.astype(jnp.float32)).astype(jnp.bfloat16)
    got_query = (got_half * own_scale * gains_in[0].astype(jnp.float32)).astype(jnp.bfloat16)
    new_keys = (key_part * key_scale * k_gain.astype(jnp.float32)).astype(jnp.bfloat16)
    new_values = value_part.astype(jnp.bfloat16)
    partner_keys = (got_keys * key_scale * gains_in[1].astype(jnp.float32)).astype(jnp.bfloat16)
    stacked = jnp.stack([new_keys, new_values], axis=1)
    partner = jnp.stack([partner_keys, got_values.astype(jnp.bfloat16)], axis=1)
    suffix_full = jnp.where(
        lower_bit == 0,
        jnp.concatenate([stacked, partner], axis=-1),
        jnp.concatenate([partner, stacked], axis=-1),
    )
    query_full = jnp.where(
        lower_bit == 0,
        jnp.concatenate([own_query, got_query], axis=-1),
        jnp.concatenate([got_query, own_query], axis=-1),
    )
    query_offset = lower_bit * half_rows
    heads_local = 1
    queries_heads = query_full.reshape(half_rows, heads_local, HD)
    groups_count = prefix_owner.shape[0]
    request_count = request_group.shape[0]
    token_group = jnp.sum(
        jnp.where(
            segments[:, None] == jnp.arange(request_count, dtype=jnp.int32)[None, :],
            request_group[None, :],
            0,
        ),
        axis=1,
    )
    base_row = seq_index * tok_seq
    query_start = base_row + query_offset
    query_seg = lax.dynamic_slice_in_dim(segments, query_start, half_rows, 0)
    query_group = lax.dynamic_slice_in_dim(token_group, query_start, half_rows, 0)
    query_pos = query_start + jnp.arange(half_rows, dtype=jnp.int32)
    padded_seg = jnp.concatenate([jnp.full((tok_seq,), -1, jnp.int32), segments], axis=0)
    key_seg = lax.dynamic_slice_in_dim(padded_seg, base_row, 2 * tok_seq, 0)
    key_pos = base_row - tok_seq + jnp.arange(2 * tok_seq, dtype=jnp.int32)
    previous = passed_along(suffix_full, "seq", 1)
    suffix_keys = jnp.concatenate([previous, suffix_full], axis=0)
    suffix_mask = (key_seg[None, :] == query_seg[:, None]) & (
        key_pos[None, :] <= query_pos[:, None]
    )
    carry = (
        jnp.full((heads_local, half_rows), -1e30, jnp.float32),
        jnp.zeros((heads_local, half_rows), jnp.float32),
        jnp.zeros((heads_local, half_rows, HD), jnp.float32),
    )
    carry = attend_block(carry, queries_heads, suffix_keys, suffix_mask)
    owner_of_query = jnp.sum(
        jnp.where(
            query_group[:, None] == jnp.arange(groups_count, dtype=jnp.int32)[None, :],
            prefix_owner[None, :],
            0,
        ),
        axis=1,
    )
    state = carry
    start = jnp.int32(0)
    for offset in range(seq_size):
        slot_mask = (owner_of_query == start + offset)[:, None]
        state = attend_halves(state, queries_heads, piece[2 * offset : 2 * offset + 2], slot_mask)
    carry = state
    attended = (carry[2] / carry[1][:, :, None]).astype(jnp.bfloat16)
    attended = jnp.transpose(attended, (1, 0, 2)).reshape(half_rows, heads_local * HD)
    split_out = attended.reshape(half_rows, 2, columns)
    own_out = lax.dynamic_index_in_dim(split_out, lower_bit, 1, keepdims=False)
    send_out = lax.dynamic_index_in_dim(split_out, 1 - lower_bit, 1, keepdims=False)
    got_out = from_partner(send_out)
    attended_local = jnp.where(
        lower_bit == 0,
        jnp.concatenate([own_out, got_out], axis=0),
        jnp.concatenate([got_out, own_out], axis=0),
    )
    attn_partial = jnp.dot(attended_local, w_out, preferred_element_type=jnp.float32)
    attn_partial = attn_partial.astype(jnp.bfloat16).reshape(tensor_size, tok_dev, width)
    attn_sum = jnp.sum(
        lax.all_to_all(attn_partial, TENSOR, 0, 0, tiled=True).astype(jnp.float32), axis=0
    )
    mixed_rows = (tokens.astype(jnp.float32) + attn_sum).astype(jnp.bfloat16)
    expert_in = rms_scale(mixed_rows.astype(jnp.float32), mlp_gain).astype(jnp.bfloat16)
    exp_local = EXP_DEV
    experts_all = exp_local * tensor_size
    capacity = max(2, 2 * tok_dev * TOP // experts_all)
    flat_ids = expert_ids.reshape(-1)
    onehot = (flat_ids[:, None] == jnp.arange(experts_all, dtype=jnp.int32)[None, :]).astype(
        jnp.int32
    )
    before = jnp.cumsum(onehot, axis=0) - onehot
    slot = flat_ids * capacity + jnp.sum(before * onehot, axis=1)
    slot_match = (
        slot.reshape(tok_dev, TOP)[:, :, None]
        == jnp.arange(experts_all * capacity, dtype=jnp.int32)[None, None, :]
    )
    dispatch_table = jnp.transpose(jnp.any(slot_match, axis=1)).astype(jnp.bfloat16)
    combine_table = jnp.sum(jnp.where(slot_match, gate_weights[:, :, None], 0.0), axis=1)
    buffer = jnp.dot(dispatch_table, expert_in, preferred_element_type=jnp.float32).astype(
        jnp.bfloat16
    )
    buffer = buffer.reshape(tensor_size, exp_local, capacity, width)
    received = lax.all_to_all(buffer, TENSOR, split_axis=0, concat_axis=0, tiled=True)
    gate_local = w_gate[0]
    up_local = w_up[0]
    down_local = w_down[0]
    holders = seq_size // exp_local
    per_expert = jnp.transpose(received, (1, 0, 2, 3))
    chosen = lax.all_to_all(jnp.repeat(per_expert, holders, axis=0), "seq", 0, 0, tiled=True)
    gated = jnp.einsum("srcd,df->srcf", chosen, gate_local, preferred_element_type=jnp.float32)
    upward = jnp.einsum("srcd,df->srcf", chosen, up_local, preferred_element_type=jnp.float32)
    activity = (jax.nn.silu(gated) * upward).astype(jnp.bfloat16)
    result = jnp.einsum("srcf,fd->srcd", activity, down_local, preferred_element_type=jnp.float32)
    back = lax.all_to_all(result.astype(jnp.bfloat16), "seq", 0, 0, tiled=True)
    summed = jnp.sum(
        back.astype(jnp.float32).reshape((exp_local, holders) + back.shape[1:]), axis=1
    )
    summed = jnp.transpose(summed, (1, 0, 2, 3))
    returned = lax.all_to_all(
        summed.astype(jnp.bfloat16), TENSOR, split_axis=0, concat_axis=0, tiled=True
    ).astype(jnp.float32)
    moe_sum = jnp.dot(
        combine_table,
        returned.reshape(experts_all * capacity, width),
        preferred_element_type=jnp.float32,
        precision=lax.Precision.HIGHEST,
    )
    output = (mixed_rows.astype(jnp.float32) + moe_sum).astype(jnp.bfloat16)
    return (output, new_keys, new_values)


def solution(mesh):
    seq_size, tensor_size = mesh.devices.shape
    grid = Mesh(mesh.devices.reshape(seq_size, tensor_size // 2, 2), ("seq",) + TENSOR)
    return jax.shard_map(
        local,
        mesh=grid,
        in_specs=(
            P(("seq",) + TENSOR, None),
            P(),
            P(None, None, TENSOR),
            P(TENSOR),
            P(TENSOR),
            P(TENSOR, None),
            P("seq", None, TENSOR),
            P("seq", None, TENSOR),
            P(),
            P(),
            P(),
            P(),
            P(("seq",) + TENSOR, None),
            P(("seq",) + TENSOR, None),
            P(TENSOR + ("seq",), None, None),
            P(TENSOR + ("seq",), None, None),
            P(TENSOR + ("seq",), None, None),
        ),
        out_specs=(P(("seq",) + TENSOR, None), P("seq", TENSOR), P("seq", TENSOR)),
        check_vma=False,
    )
```

```python
import jax
import jax.numpy as jnp
from jax import lax
from jax.sharding import Mesh
from jax.sharding import PartitionSpec as P

HD = 128
TOP = 8
EXP_DEV = 2
TENSOR = ("th", "tyl")


def from_partner(value):
    return lax.ppermute(value, "tyl", [(0, 1), (1, 0)])


def passed_along(value, axis, by):
    devices = lax.axis_size(axis)
    pairs = [(i, i + by) for i in range(devices) if 0 <= i + by < devices]
    return lax.ppermute(value, axis, pairs)


def gather_by_exchange(value, axis):
    devices = lax.axis_size(axis)
    copies = jnp.broadcast_to(value[None], (devices,) + value.shape)
    got = lax.all_to_all(copies, axis, 0, 0, tiled=True)
    return got


def rms_scale(values, gain):
    mean_square = jnp.mean(values * values, axis=-1, keepdims=True)
    return values * lax.rsqrt(mean_square + 1e-05) * gain.astype(jnp.float32)


def attend_block(carry, queries_heads, block, mask):
    largest, total, accum = carry
    heads_local = queries_heads.shape[1]
    count = block.shape[0]
    key_block = block[:, 0].reshape(count, heads_local, HD)
    value_block = block[:, 1].reshape(count, heads_local, HD)
    scores = jnp.einsum(
        "qhd,khd->hqk", queries_heads, key_block, preferred_element_type=jnp.float32
    ) * HD ** (-0.5)
    scores = jnp.where(mask[None], scores, -1e30)
    new_largest = jnp.maximum(largest, jnp.max(scores, axis=-1))
    weights = jnp.where(mask[None], jnp.exp(scores - new_largest[:, :, None]), 0.0)
    factor = jnp.exp(largest - new_largest)
    total = total * factor + jnp.sum(weights, axis=-1)
    update = jnp.einsum(
        "hqk,khd->hqd",
        weights.astype(jnp.bfloat16),
        value_block,
        preferred_element_type=jnp.float32,
    )
    accum = accum * factor[:, :, None] + update
    return (new_largest, total, accum)


def attend_halves(carry, queries_heads, halves, mask):
    largest, total, accum = carry
    rows = queries_heads.shape[0]
    split_queries = queries_heads.reshape(rows, 2, HD // 2)
    scores = jnp.einsum(
        "qcd,ckd->qk", split_queries, halves[..., : HD // 2], preferred_element_type=jnp.float32
    )[None] * HD ** (-0.5)
    scores = jnp.where(mask[None], scores, -1e30)
    new_largest = jnp.maximum(largest, jnp.max(scores, axis=-1))
    weights = jnp.where(mask[None], jnp.exp(scores - new_largest[:, :, None]), 0.0)
    factor = jnp.exp(largest - new_largest)
    total = total * factor + jnp.sum(weights, axis=-1)
    update = jnp.einsum(
        "qk,ckd->qcd",
        weights[0].astype(jnp.bfloat16),
        halves[..., HD // 2 :],
        preferred_element_type=jnp.float32,
    ).reshape(1, rows, HD)
    accum = accum * factor[:, :, None] + update
    return (new_largest, total, accum)


def local(
    tokens,
    attn_gain,
    w_qkv,
    q_gain,
    k_gain,
    w_out,
    prefix_keys,
    prefix_values,
    segments,
    request_group,
    prefix_owner,
    mlp_gain,
    expert_ids,
    gate_weights,
    w_gate,
    w_up,
    w_down,
):
    tensor_size = lax.axis_size(TENSOR)
    seq_size = lax.axis_size("seq")
    seq_index = lax.axis_index("seq")
    tensor_index = lax.axis_index(TENSOR)
    tok_dev = tokens.shape[0]
    width = tokens.shape[1]
    tok_seq = tok_dev * tensor_size
    columns = w_qkv.shape[2]
    lower_bit = tensor_index % 2
    prefix_own = jnp.concatenate([prefix_keys[0], prefix_values[0]], axis=-1)
    piece = lax.all_gather(prefix_own[None], ("seq", "tyl"), axis=0, tiled=True)
    gains_in = from_partner(jnp.stack([q_gain, k_gain]))
    normed = rms_scale(tokens.astype(jnp.float32), attn_gain).astype(jnp.bfloat16)
    w_flat = w_qkv.reshape(width, 3 * columns)
    rows = gather_by_exchange(normed, TENSOR).reshape(tok_seq, width)
    projected = jnp.dot(
        rows,
        w_flat,
        preferred_element_type=jnp.float32,
    )
    query_part = projected[:, :columns]
    key_part = projected[:, columns : 2 * columns]
    value_part = projected[:, 2 * columns :]
    partial_squares = jnp.stack(
        [jnp.sum(query_part * query_part, axis=-1), jnp.sum(key_part * key_part, axis=-1)]
    )
    half_rows = tok_seq // 2
    query_halves = query_part.reshape(2, half_rows, columns)
    own_half = lax.dynamic_index_in_dim(query_halves, lower_bit, 0, keepdims=False)
    send_half = lax.dynamic_index_in_dim(query_halves, 1 - lower_bit, 0, keepdims=False)
    raw_out = jnp.concatenate([send_half, key_part, value_part], axis=0)
    raw_out, partial_squares = lax.optimization_barrier((raw_out, partial_squares))
    raw_in = from_partner(raw_out)
    got_half = raw_in[:half_rows]
    got_keys = raw_in[half_rows : half_rows + tok_seq]
    got_values = raw_in[half_rows + tok_seq :]
    squares = jnp.sum(gather_by_exchange(partial_squares, TENSOR), axis=0)
    query_scale = lax.rsqrt(squares[0] / width + 1e-05)[:, None]
    key_scale = lax.rsqrt(squares[1] / width + 1e-05)[:, None]
    own_scale = lax.dynamic_index_in_dim(
        query_scale.reshape(2, half_rows, 1), lower_bit, 0, keepdims=False
    )
    own_query = (own_half * own_scale * q_gain.astype(jnp.float32)).astype(jnp.bfloat16)
    got_query = (got_half * own_scale * gains_in[0].astype(jnp.float32)).astype(jnp.bfloat16)
    new_keys = (key_part * key_scale * k_gain.astype(jnp.float32)).astype(jnp.bfloat16)
    new_values = value_part.astype(jnp.bfloat16)
    partner_keys = (got_keys * key_scale * gains_in[1].astype(jnp.float32)).astype(jnp.bfloat16)
    stacked = jnp.stack([new_keys, new_values], axis=1)
    partner = jnp.stack([partner_keys, got_values.astype(jnp.bfloat16)], axis=1)
    suffix_full = jnp.where(
        lower_bit == 0,
        jnp.concatenate([stacked, partner], axis=-1),
        jnp.concatenate([partner, stacked], axis=-1),
    )
    query_full = jnp.where(
        lower_bit == 0,
        jnp.concatenate([own_query, got_query], axis=-1),
        jnp.concatenate([got_query, own_query], axis=-1),
    )
    query_offset = lower_bit * half_rows
    heads_local = 1
    queries_heads = query_full.reshape(half_rows, heads_local, HD)
    groups_count = prefix_owner.shape[0]
    request_count = request_group.shape[0]
    token_group = jnp.sum(
        jnp.where(
            segments[:, None] == jnp.arange(request_count, dtype=jnp.int32)[None, :],
            request_group[None, :],
            0,
        ),
        axis=1,
    )
    base_row = seq_index * tok_seq
    query_start = base_row + query_offset
    query_seg = lax.dynamic_slice_in_dim(segments, query_start, half_rows, 0)
    query_group = lax.dynamic_slice_in_dim(token_group, query_start, half_rows, 0)
    query_pos = query_start + jnp.arange(half_rows, dtype=jnp.int32)
    padded_seg = jnp.concatenate([jnp.full((tok_seq,), -1, jnp.int32), segments], axis=0)
    key_seg = lax.dynamic_slice_in_dim(padded_seg, base_row, 2 * tok_seq, 0)
    key_pos = base_row - tok_seq + jnp.arange(2 * tok_seq, dtype=jnp.int32)
    previous = passed_along(suffix_full, "seq", 1)
    suffix_keys = jnp.concatenate([previous, suffix_full], axis=0)
    suffix_mask = (key_seg[None, :] == query_seg[:, None]) & (
        key_pos[None, :] <= query_pos[:, None]
    )
    carry = (
        jnp.full((heads_local, half_rows), -1e30, jnp.float32),
        jnp.zeros((heads_local, half_rows), jnp.float32),
        jnp.zeros((heads_local, half_rows, HD), jnp.float32),
    )
    carry = attend_block(carry, queries_heads, suffix_keys, suffix_mask)
    owner_of_query = jnp.sum(
        jnp.where(
            query_group[:, None] == jnp.arange(groups_count, dtype=jnp.int32)[None, :],
            prefix_owner[None, :],
            0,
        ),
        axis=1,
    )
    state = carry
    start = jnp.int32(0)
    for offset in range(seq_size):
        slot_mask = (owner_of_query == start + offset)[:, None]
        state = attend_halves(state, queries_heads, piece[2 * offset : 2 * offset + 2], slot_mask)
    carry = state
    attended = (carry[2] / carry[1][:, :, None]).astype(jnp.bfloat16)
    attended = jnp.transpose(attended, (1, 0, 2)).reshape(half_rows, heads_local * HD)
    split_out = attended.reshape(half_rows, 2, columns)
    own_out = lax.dynamic_index_in_dim(split_out, lower_bit, 1, keepdims=False)
    send_out = lax.dynamic_index_in_dim(split_out, 1 - lower_bit, 1, keepdims=False)
    got_out = from_partner(send_out)
    attended_local = jnp.where(
        lower_bit == 0,
        jnp.concatenate([own_out, got_out], axis=0),
        jnp.concatenate([got_out, own_out], axis=0),
    )
    attn_partial = jnp.dot(attended_local, w_out, preferred_element_type=jnp.float32)
    attn_partial = attn_partial.astype(jnp.bfloat16).reshape(tensor_size, tok_dev, width)
    attn_sum = jnp.sum(
        lax.all_to_all(attn_partial, TENSOR, 0, 0, tiled=True).astype(jnp.float32), axis=0
    )
    mixed_rows = (tokens.astype(jnp.float32) + attn_sum).astype(jnp.bfloat16)
    expert_in = rms_scale(mixed_rows.astype(jnp.float32), mlp_gain).astype(jnp.bfloat16)
    exp_local = EXP_DEV
    experts_all = exp_local * tensor_size
    capacity = max(2, 2 * tok_dev * TOP // experts_all)
    flat_ids = expert_ids.reshape(-1)
    onehot = (flat_ids[:, None] == jnp.arange(experts_all, dtype=jnp.int32)[None, :]).astype(
        jnp.int32
    )
    before = jnp.cumsum(onehot, axis=0) - onehot
    slot = flat_ids * capacity + jnp.sum(before * onehot, axis=1)
    slot_match = (
        slot.reshape(tok_dev, TOP)[:, :, None]
        == jnp.arange(experts_all * capacity, dtype=jnp.int32)[None, None, :]
    )
    dispatch_table = jnp.transpose(jnp.any(slot_match, axis=1)).astype(jnp.bfloat16)
    combine_table = jnp.sum(jnp.where(slot_match, gate_weights[:, :, None], 0.0), axis=1)
    buffer = jnp.dot(dispatch_table, expert_in, preferred_element_type=jnp.float32).astype(
        jnp.bfloat16
    )
    buffer = buffer.reshape(tensor_size, exp_local, capacity, width)
    received = lax.all_to_all(buffer, TENSOR, split_axis=0, concat_axis=0, tiled=True)
    gate_local = w_gate[0]
    up_local = w_up[0]
    down_local = w_down[0]
    holders = seq_size // exp_local
    per_expert = jnp.transpose(received, (1, 0, 2, 3))
    chosen = lax.all_to_all(jnp.repeat(per_expert, holders, axis=0), "seq", 0, 0, tiled=True)
    gated = jnp.einsum("srcd,df->srcf", chosen, gate_local, preferred_element_type=jnp.float32)
    upward = jnp.einsum("srcd,df->srcf", chosen, up_local, preferred_element_type=jnp.float32)
    activity = (jax.nn.silu(gated) * upward).astype(jnp.bfloat16)
    result = jnp.einsum("srcf,fd->srcd", activity, down_local, preferred_element_type=jnp.float32)
    back = lax.all_to_all(result.astype(jnp.bfloat16), "seq", 0, 0, tiled=True)
    summed = jnp.sum(
        back.astype(jnp.float32).reshape((exp_local, holders) + back.shape[1:]), axis=1
    )
    summed = jnp.transpose(summed, (1, 0, 2, 3))
    returned = lax.all_to_all(
        summed.astype(jnp.bfloat16), TENSOR, split_axis=0, concat_axis=0, tiled=True
    ).astype(jnp.float32)
    moe_sum = jnp.dot(
        combine_table,
        returned.reshape(experts_all * capacity, width),
        preferred_element_type=jnp.float32,
        precision=lax.Precision.HIGHEST,
    )
    output = (mixed_rows.astype(jnp.float32) + moe_sum).astype(jnp.bfloat16)
    return (output, new_keys, new_values)


def solution(mesh):
    seq_size, tensor_size = mesh.devices.shape
    grid = Mesh(mesh.devices.reshape(seq_size, tensor_size // 2, 2), ("seq",) + TENSOR)
    return jax.shard_map(
        local,
        mesh=grid,
        in_specs=(
            P(("seq",) + TENSOR, None),
            P(),
            P(None, None, TENSOR),
            P(TENSOR),
            P(TENSOR),
            P(TENSOR, None),
            P("seq", None, TENSOR),
            P("seq", None, TENSOR),
            P(),
            P(),
            P(),
            P(),
            P(("seq",) + TENSOR, None),
            P(("seq",) + TENSOR, None),
            P(TENSOR + ("seq",), None, None),
            P(TENSOR + ("seq",), None, None),
            P(TENSOR + ("seq",), None, None),
        ),
        out_specs=(P(("seq",) + TENSOR, None), P("seq", TENSOR), P("seq", TENSOR)),
        check_vma=False,
    )
```

```python
import jax
import jax.numpy as jnp
from jax import lax
from jax.sharding import Mesh
from jax.sharding import PartitionSpec as P

HD = 128
TOP = 8
EXP_DEV = 2
TENSOR = ("th", "tyl")


def from_partner(value):
    return lax.ppermute(value, "tyl", [(0, 1), (1, 0)])


def passed_along(value, axis, by):
    devices = lax.axis_size(axis)
    pairs = [(i, i + by) for i in range(devices) if 0 <= i + by < devices]
    return lax.ppermute(value, axis, pairs)


def gather_by_exchange(value, axis):
    devices = lax.axis_size(axis)
    copies = jnp.broadcast_to(value[None], (devices,) + value.shape)
    got = lax.all_to_all(copies, axis, 0, 0, tiled=True)
    return got


def rms_scale(values, gain):
    mean_square = jnp.mean(values * values, axis=-1, keepdims=True)
    return values * lax.rsqrt(mean_square + 1e-05) * gain.astype(jnp.float32)


def attend_block(carry, queries_heads, block, mask):
    largest, total, accum = carry
    heads_local = queries_heads.shape[1]
    count = block.shape[0]
    key_block = block[:, 0].reshape(count, heads_local, HD)
    value_block = block[:, 1].reshape(count, heads_local, HD)
    scores = jnp.einsum(
        "qhd,khd->hqk", queries_heads, key_block, preferred_element_type=jnp.float32
    ) * HD ** (-0.5)
    scores = jnp.where(mask[None], scores, -1e30)
    new_largest = jnp.maximum(largest, jnp.max(scores, axis=-1))
    weights = jnp.where(mask[None], jnp.exp(scores - new_largest[:, :, None]), 0.0)
    factor = jnp.exp(largest - new_largest)
    total = total * factor + jnp.sum(weights, axis=-1)
    update = jnp.einsum(
        "hqk,khd->hqd",
        weights.astype(jnp.bfloat16),
        value_block,
        preferred_element_type=jnp.float32,
    )
    accum = accum * factor[:, :, None] + update
    return (new_largest, total, accum)


def local(
    tokens,
    attn_gain,
    w_qkv,
    q_gain,
    k_gain,
    w_out,
    prefix_keys,
    prefix_values,
    segments,
    request_group,
    prefix_owner,
    mlp_gain,
    expert_ids,
    gate_weights,
    w_gate,
    w_up,
    w_down,
):
    tensor_size = lax.axis_size(TENSOR)
    seq_size = lax.axis_size("seq")
    seq_index = lax.axis_index("seq")
    tensor_index = lax.axis_index(TENSOR)
    tok_dev = tokens.shape[0]
    width = tokens.shape[1]
    tok_seq = tok_dev * tensor_size
    columns = w_qkv.shape[2]
    lower_bit = tensor_index % 2
    prefix_own = jnp.stack([prefix_keys[0], prefix_values[0]], axis=1)
    prefix_partner = from_partner(prefix_own)
    prefix_full = jnp.where(
        lower_bit == 0,
        jnp.concatenate([prefix_own, prefix_partner], axis=-1),
        jnp.concatenate([prefix_partner, prefix_own], axis=-1),
    )
    piece = lax.all_gather(prefix_full[None], "seq", axis=0, tiled=True)
    gains_in = from_partner(jnp.stack([q_gain, k_gain]))
    out_partner = from_partner(w_out)
    out_head = jnp.where(
        lower_bit == 0,
        jnp.concatenate([w_out, out_partner], axis=0),
        jnp.concatenate([out_partner, w_out], axis=0),
    )
    normed = rms_scale(tokens.astype(jnp.float32), attn_gain).astype(jnp.bfloat16)
    w_flat = w_qkv.reshape(width, 3 * columns)
    rows = gather_by_exchange(normed, TENSOR).reshape(tok_seq, width)
    projected = jnp.dot(
        rows,
        w_flat,
        preferred_element_type=jnp.float32,
    )
    query_part = projected[:, :columns]
    key_part = projected[:, columns : 2 * columns]
    value_part = projected[:, 2 * columns :]
    partial_squares = jnp.stack(
        [jnp.sum(query_part * query_part, axis=-1), jnp.sum(key_part * key_part, axis=-1)]
    )
    half_rows = tok_seq // 2
    row_blocks = half_rows // tok_dev

    def own_rows(values, mine=True):
        blocks = values.reshape((row_blocks, 2, tok_dev) + values.shape[1:])
        first, second = (blocks[:, 0], blocks[:, 1]) if mine else (blocks[:, 1], blocks[:, 0])
        return jnp.where(lower_bit == 0, first, second).reshape((half_rows,) + values.shape[1:])

    own_half = own_rows(query_part)
    send_half = own_rows(query_part, mine=False)
    raw_out = jnp.concatenate([send_half, key_part, value_part], axis=0)
    raw_out, partial_squares = lax.optimization_barrier((raw_out, partial_squares))
    raw_in = from_partner(raw_out)
    got_half = raw_in[:half_rows]
    got_keys = raw_in[half_rows : half_rows + tok_seq]
    got_values = raw_in[half_rows + tok_seq :]
    squares = jnp.sum(gather_by_exchange(partial_squares, TENSOR), axis=0)
    query_scale = lax.rsqrt(squares[0] / width + 1e-05)[:, None]
    key_scale = lax.rsqrt(squares[1] / width + 1e-05)[:, None]
    own_scale = own_rows(query_scale)
    own_query = (own_half * own_scale * q_gain.astype(jnp.float32)).astype(jnp.bfloat16)
    got_query = (got_half * own_scale * gains_in[0].astype(jnp.float32)).astype(jnp.bfloat16)
    new_keys = (key_part * key_scale * k_gain.astype(jnp.float32)).astype(jnp.bfloat16)
    new_values = value_part.astype(jnp.bfloat16)
    partner_keys = (got_keys * key_scale * gains_in[1].astype(jnp.float32)).astype(jnp.bfloat16)
    stacked = jnp.stack([new_keys, new_values], axis=1)
    partner = jnp.stack([partner_keys, got_values.astype(jnp.bfloat16)], axis=1)
    suffix_full = jnp.where(
        lower_bit == 0,
        jnp.concatenate([stacked, partner], axis=-1),
        jnp.concatenate([partner, stacked], axis=-1),
    )
    query_full = jnp.where(
        lower_bit == 0,
        jnp.concatenate([own_query, got_query], axis=-1),
        jnp.concatenate([got_query, own_query], axis=-1),
    )
    heads_local = 1
    queries_heads = query_full.reshape(half_rows, heads_local, HD)
    groups_count = prefix_owner.shape[0]
    request_count = request_group.shape[0]
    token_group = jnp.sum(
        jnp.where(
            segments[:, None] == jnp.arange(request_count, dtype=jnp.int32)[None, :],
            request_group[None, :],
            0,
        ),
        axis=1,
    )
    base_row = seq_index * tok_seq
    query_seg = own_rows(lax.dynamic_slice_in_dim(segments, base_row, tok_seq, 0))
    query_group = own_rows(lax.dynamic_slice_in_dim(token_group, base_row, tok_seq, 0))
    query_pos = own_rows(base_row + jnp.arange(tok_seq, dtype=jnp.int32))
    padded_seg = jnp.concatenate([jnp.full((tok_seq,), -1, jnp.int32), segments], axis=0)
    key_seg = lax.dynamic_slice_in_dim(padded_seg, base_row, 2 * tok_seq, 0)
    key_pos = base_row - tok_seq + jnp.arange(2 * tok_seq, dtype=jnp.int32)
    previous = passed_along(suffix_full, "seq", 1)
    suffix_keys = jnp.concatenate([previous, suffix_full], axis=0)
    suffix_mask = (key_seg[None, :] == query_seg[:, None]) & (
        key_pos[None, :] <= query_pos[:, None]
    )
    carry = (
        jnp.full((heads_local, half_rows), -1e30, jnp.float32),
        jnp.zeros((heads_local, half_rows), jnp.float32),
        jnp.zeros((heads_local, half_rows, HD), jnp.float32),
    )
    carry = attend_block(carry, queries_heads, suffix_keys, suffix_mask)
    owner_of_query = jnp.sum(
        jnp.where(
            query_group[:, None] == jnp.arange(groups_count, dtype=jnp.int32)[None, :],
            prefix_owner[None, :],
            0,
        ),
        axis=1,
    )
    state = carry
    start = jnp.int32(0)
    for offset in range(piece.shape[0]):
        slot_mask = (owner_of_query == start + offset)[:, None]
        state = attend_block(state, queries_heads, piece[offset], slot_mask)
    carry = state
    attended = (carry[2] / carry[1][:, :, None]).astype(jnp.bfloat16)
    attended = jnp.transpose(attended, (1, 0, 2)).reshape(half_rows, heads_local * HD)
    attn_partial = jnp.dot(attended, out_head, preferred_element_type=jnp.float32)
    attn_partial = attn_partial.astype(jnp.bfloat16).reshape(row_blocks, tok_dev, width)
    attn_sum = jnp.sum(
        lax.all_to_all(attn_partial, "th", 0, 0, tiled=True).astype(jnp.float32), axis=0
    )
    mixed_rows = (tokens.astype(jnp.float32) + attn_sum).astype(jnp.bfloat16)
    expert_in = rms_scale(mixed_rows.astype(jnp.float32), mlp_gain).astype(jnp.bfloat16)
    exp_local = EXP_DEV
    experts_all = exp_local * tensor_size
    capacity = max(2, 2 * tok_dev * TOP // experts_all)
    flat_ids = expert_ids.reshape(-1)
    onehot = (flat_ids[:, None] == jnp.arange(experts_all, dtype=jnp.int32)[None, :]).astype(
        jnp.int32
    )
    before = jnp.cumsum(onehot, axis=0) - onehot
    slot = flat_ids * capacity + jnp.sum(before * onehot, axis=1)
    slot_match = (
        slot.reshape(tok_dev, TOP)[:, :, None]
        == jnp.arange(experts_all * capacity, dtype=jnp.int32)[None, None, :]
    )
    dispatch_table = jnp.transpose(jnp.any(slot_match, axis=1)).astype(jnp.bfloat16)
    combine_table = jnp.sum(jnp.where(slot_match, gate_weights[:, :, None], 0.0), axis=1)
    buffer = jnp.dot(dispatch_table, expert_in, preferred_element_type=jnp.float32).astype(
        jnp.bfloat16
    )
    buffer = buffer.reshape(tensor_size, exp_local, capacity, width)
    received = lax.all_to_all(buffer, TENSOR, split_axis=0, concat_axis=0, tiled=True)
    gate_local = w_gate[0]
    up_local = w_up[0]
    down_local = w_down[0]
    holders = seq_size // exp_local
    per_expert = jnp.transpose(received, (1, 0, 2, 3))
    chosen = lax.all_to_all(jnp.repeat(per_expert, holders, axis=0), "seq", 0, 0, tiled=True)
    gated = jnp.einsum("srcd,df->srcf", chosen, gate_local, preferred_element_type=jnp.float32)
    upward = jnp.einsum("srcd,df->srcf", chosen, up_local, preferred_element_type=jnp.float32)
    activity = (jax.nn.silu(gated) * upward).astype(jnp.bfloat16)
    result = jnp.einsum("srcf,fd->srcd", activity, down_local, preferred_element_type=jnp.float32)
    back = lax.all_to_all(result.astype(jnp.bfloat16), "seq", 0, 0, tiled=True)
    summed = jnp.sum(
        back.astype(jnp.float32).reshape((exp_local, holders) + back.shape[1:]), axis=1
    )
    summed = jnp.transpose(summed, (1, 0, 2, 3))
    returned = lax.all_to_all(
        summed.astype(jnp.bfloat16), TENSOR, split_axis=0, concat_axis=0, tiled=True
    ).astype(jnp.float32)
    moe_sum = jnp.dot(
        combine_table,
        returned.reshape(experts_all * capacity, width),
        preferred_element_type=jnp.float32,
        precision=lax.Precision.HIGHEST,
    )
    output = (mixed_rows.astype(jnp.float32) + moe_sum).astype(jnp.bfloat16)
    return (output, new_keys, new_values)


def solution(mesh):
    seq_size, tensor_size = mesh.devices.shape
    grid = Mesh(mesh.devices.reshape(seq_size, tensor_size // 2, 2), ("seq",) + TENSOR)
    return jax.shard_map(
        local,
        mesh=grid,
        in_specs=(
            P(("seq",) + TENSOR, None),
            P(),
            P(None, None, TENSOR),
            P(TENSOR),
            P(TENSOR),
            P(TENSOR, None),
            P("seq", None, TENSOR),
            P("seq", None, TENSOR),
            P(),
            P(),
            P(),
            P(),
            P(("seq",) + TENSOR, None),
            P(("seq",) + TENSOR, None),
            P(TENSOR + ("seq",), None, None),
            P(TENSOR + ("seq",), None, None),
            P(TENSOR + ("seq",), None, None),
        ),
        out_specs=(P(("seq",) + TENSOR, None), P("seq", TENSOR), P("seq", TENSOR)),
        check_vma=False,
    )
```

```python
import jax
import jax.numpy as jnp
from jax import lax
from jax.sharding import Mesh
from jax.sharding import PartitionSpec as P

HD = 128
TOP = 8
EXP_DEV = 2
TENSOR = ("th", "tyl")
SEQ = ("sx", "sc")


def from_partner(value):
    return lax.ppermute(value, "tyl", [(0, 1), (1, 0)])


def passed_along(value, axis, by):
    devices = lax.axis_size(axis)
    pairs = [(i, i + by) for i in range(devices) if 0 <= i + by < devices]
    return lax.ppermute(value, axis, pairs)


def gather_by_exchange(value, axis):
    devices = lax.axis_size(axis)
    copies = jnp.broadcast_to(value[None], (devices,) + value.shape)
    got = lax.all_to_all(copies, axis, 0, 0, tiled=True)
    return got


def rms_scale(values, gain):
    mean_square = jnp.mean(values * values, axis=-1, keepdims=True)
    return values * lax.rsqrt(mean_square + 1e-05) * gain.astype(jnp.float32)


def attend_block(carry, queries_heads, block, mask):
    largest, total, accum = carry
    heads_local = queries_heads.shape[1]
    count = block.shape[0]
    key_block = block[:, 0].reshape(count, heads_local, HD)
    value_block = block[:, 1].reshape(count, heads_local, HD)
    scores = jnp.einsum(
        "qhd,khd->hqk", queries_heads, key_block, preferred_element_type=jnp.float32
    ) * HD ** (-0.5)
    scores = jnp.where(mask[None], scores, -1e30)
    new_largest = jnp.maximum(largest, jnp.max(scores, axis=-1))
    weights = jnp.where(mask[None], jnp.exp(scores - new_largest[:, :, None]), 0.0)
    factor = jnp.exp(largest - new_largest)
    total = total * factor + jnp.sum(weights, axis=-1)
    update = jnp.einsum(
        "hqk,khd->hqd",
        weights.astype(jnp.bfloat16),
        value_block,
        preferred_element_type=jnp.float32,
    )
    accum = accum * factor[:, :, None] + update
    return (new_largest, total, accum)


def local(
    tokens,
    attn_gain,
    w_qkv,
    q_gain,
    k_gain,
    w_out,
    prefix_keys,
    prefix_values,
    segments,
    request_group,
    prefix_owner,
    mlp_gain,
    expert_ids,
    gate_weights,
    w_gate,
    w_up,
    w_down,
):
    tensor_size = lax.axis_size(TENSOR)
    seq_size = lax.axis_size(SEQ)
    seq_index = lax.axis_index(SEQ)
    tensor_index = lax.axis_index(TENSOR)
    tok_dev = tokens.shape[0]
    width = tokens.shape[1]
    tok_seq = tok_dev * tensor_size
    columns = w_qkv.shape[2]
    lower_bit = tensor_index % 2
    prefix_own = jnp.stack([prefix_keys[0], prefix_values[0]], axis=1)
    prefix_partner = from_partner(prefix_own)
    prefix_full = jnp.where(
        lower_bit == 0,
        jnp.concatenate([prefix_own, prefix_partner], axis=-1),
        jnp.concatenate([prefix_partner, prefix_own], axis=-1),
    )
    piece = lax.all_gather(prefix_full[None], SEQ, axis=0, tiled=True)
    gains_in = from_partner(jnp.stack([q_gain, k_gain]))
    out_partner = from_partner(w_out)
    out_head = jnp.where(
        lower_bit == 0,
        jnp.concatenate([w_out, out_partner], axis=0),
        jnp.concatenate([out_partner, w_out], axis=0),
    )
    normed = rms_scale(tokens.astype(jnp.float32), attn_gain).astype(jnp.bfloat16)
    w_flat = w_qkv.reshape(width, 3 * columns)
    rows = gather_by_exchange(normed, TENSOR).reshape(tok_seq, width)
    projected = jnp.dot(
        rows,
        w_flat,
        preferred_element_type=jnp.float32,
    )
    query_part = projected[:, :columns]
    key_part = projected[:, columns : 2 * columns]
    value_part = projected[:, 2 * columns :]
    partial_squares = jnp.stack(
        [jnp.sum(query_part * query_part, axis=-1), jnp.sum(key_part * key_part, axis=-1)]
    )
    half_rows = tok_seq // 2
    row_blocks = half_rows // tok_dev

    def own_rows(values, mine=True):
        blocks = values.reshape((row_blocks, 2, tok_dev) + values.shape[1:])
        first, second = (blocks[:, 0], blocks[:, 1]) if mine else (blocks[:, 1], blocks[:, 0])
        return jnp.where(lower_bit == 0, first, second).reshape((half_rows,) + values.shape[1:])

    own_half = own_rows(query_part)
    send_half = own_rows(query_part, mine=False)
    raw_out = jnp.concatenate([send_half, key_part, value_part], axis=0)
    raw_out, partial_squares = lax.optimization_barrier((raw_out, partial_squares))
    raw_in = from_partner(raw_out)
    got_half = raw_in[:half_rows]
    got_keys = raw_in[half_rows : half_rows + tok_seq]
    got_values = raw_in[half_rows + tok_seq :]
    squares = jnp.sum(gather_by_exchange(partial_squares, TENSOR), axis=0)
    query_scale = lax.rsqrt(squares[0] / width + 1e-05)[:, None]
    key_scale = lax.rsqrt(squares[1] / width + 1e-05)[:, None]
    own_scale = own_rows(query_scale)
    own_query = (own_half * own_scale * q_gain.astype(jnp.float32)).astype(jnp.bfloat16)
    got_query = (got_half * own_scale * gains_in[0].astype(jnp.float32)).astype(jnp.bfloat16)
    new_keys = (key_part * key_scale * k_gain.astype(jnp.float32)).astype(jnp.bfloat16)
    new_values = value_part.astype(jnp.bfloat16)
    partner_keys = (got_keys * key_scale * gains_in[1].astype(jnp.float32)).astype(jnp.bfloat16)
    stacked = jnp.stack([new_keys, new_values], axis=1)
    partner = jnp.stack([partner_keys, got_values.astype(jnp.bfloat16)], axis=1)
    suffix_full = jnp.where(
        lower_bit == 0,
        jnp.concatenate([stacked, partner], axis=-1),
        jnp.concatenate([partner, stacked], axis=-1),
    )
    query_full = jnp.where(
        lower_bit == 0,
        jnp.concatenate([own_query, got_query], axis=-1),
        jnp.concatenate([got_query, own_query], axis=-1),
    )
    heads_local = 1
    queries_heads = query_full.reshape(half_rows, heads_local, HD)
    groups_count = prefix_owner.shape[0]
    request_count = request_group.shape[0]
    token_group = jnp.sum(
        jnp.where(
            segments[:, None] == jnp.arange(request_count, dtype=jnp.int32)[None, :],
            request_group[None, :],
            0,
        ),
        axis=1,
    )
    base_row = seq_index * tok_seq
    query_seg = own_rows(lax.dynamic_slice_in_dim(segments, base_row, tok_seq, 0))
    query_group = own_rows(lax.dynamic_slice_in_dim(token_group, base_row, tok_seq, 0))
    query_pos = own_rows(base_row + jnp.arange(tok_seq, dtype=jnp.int32))
    padded_seg = jnp.concatenate([jnp.full((tok_seq,), -1, jnp.int32), segments], axis=0)
    key_seg = lax.dynamic_slice_in_dim(padded_seg, base_row, 2 * tok_seq, 0)
    key_pos = base_row - tok_seq + jnp.arange(2 * tok_seq, dtype=jnp.int32)
    previous = passed_along(suffix_full, SEQ, 1)
    suffix_keys = jnp.concatenate([previous, suffix_full], axis=0)
    suffix_mask = (key_seg[None, :] == query_seg[:, None]) & (
        key_pos[None, :] <= query_pos[:, None]
    )
    carry = (
        jnp.full((heads_local, half_rows), -1e30, jnp.float32),
        jnp.zeros((heads_local, half_rows), jnp.float32),
        jnp.zeros((heads_local, half_rows, HD), jnp.float32),
    )
    carry = attend_block(carry, queries_heads, suffix_keys, suffix_mask)
    owner_of_query = jnp.sum(
        jnp.where(
            query_group[:, None] == jnp.arange(groups_count, dtype=jnp.int32)[None, :],
            prefix_owner[None, :],
            0,
        ),
        axis=1,
    )
    state = carry
    start = jnp.int32(0)
    for offset in range(piece.shape[0]):
        slot_mask = (owner_of_query == start + offset)[:, None]
        state = attend_block(state, queries_heads, piece[offset], slot_mask)
    carry = state
    attended = (carry[2] / carry[1][:, :, None]).astype(jnp.bfloat16)
    attended = jnp.transpose(attended, (1, 0, 2)).reshape(half_rows, heads_local * HD)
    attn_partial = jnp.dot(attended, out_head, preferred_element_type=jnp.float32)
    attn_partial = attn_partial.astype(jnp.bfloat16).reshape(row_blocks, tok_dev, width)
    attn_sum = jnp.sum(
        lax.all_to_all(attn_partial, "th", 0, 0, tiled=True).astype(jnp.float32), axis=0
    )
    mixed_rows = (tokens.astype(jnp.float32) + attn_sum).astype(jnp.bfloat16)
    expert_in = rms_scale(mixed_rows.astype(jnp.float32), mlp_gain).astype(jnp.bfloat16)
    exp_local = EXP_DEV
    experts_all = exp_local * tensor_size
    capacity = max(2, 2 * tok_dev * TOP // experts_all)
    flat_ids = expert_ids.reshape(-1)
    onehot = (flat_ids[:, None] == jnp.arange(experts_all, dtype=jnp.int32)[None, :]).astype(
        jnp.int32
    )
    before = jnp.cumsum(onehot, axis=0) - onehot
    slot = flat_ids * capacity + jnp.sum(before * onehot, axis=1)
    slot_match = (
        slot.reshape(tok_dev, TOP)[:, :, None]
        == jnp.arange(experts_all * capacity, dtype=jnp.int32)[None, None, :]
    )
    dispatch_table = jnp.transpose(jnp.any(slot_match, axis=1)).astype(jnp.bfloat16)
    combine_table = jnp.sum(jnp.where(slot_match, gate_weights[:, :, None], 0.0), axis=1)
    buffer = jnp.dot(dispatch_table, expert_in, preferred_element_type=jnp.float32).astype(
        jnp.bfloat16
    )
    buffer = buffer.reshape(tensor_size, exp_local, capacity, width)
    received = lax.all_to_all(buffer, TENSOR, split_axis=0, concat_axis=0, tiled=True)
    gate_local = w_gate[0]
    up_local = w_up[0]
    down_local = w_down[0]
    chips = lax.axis_size("sx")
    core = lax.axis_index("sc")
    per_expert = jnp.transpose(received, (1, 0, 2, 3))
    got = lax.all_to_all(
        jnp.repeat(per_expert, chips // exp_local, axis=0), "sx", 0, 0, tiled=True
    )
    chosen = lax.all_gather(got, "sc", axis=1).reshape((seq_size,) + got.shape[1:])
    gated = jnp.einsum("srcd,df->srcf", chosen, gate_local, preferred_element_type=jnp.float32)
    upward = jnp.einsum("srcd,df->srcf", chosen, up_local, preferred_element_type=jnp.float32)
    activity = (jax.nn.silu(gated) * upward).astype(jnp.bfloat16)
    result = jnp.einsum("srcf,fd->srcd", activity, down_local, preferred_element_type=jnp.float32)
    by_core = result.astype(jnp.bfloat16).reshape((chips, 2) + result.shape[1:])
    keep = jnp.where(core == 0, by_core[:, 0], by_core[:, 1])
    give = jnp.where(core == 0, by_core[:, 1], by_core[:, 0])
    sibling = lax.ppermute(give, "sc", [(0, 1), (1, 0)])
    pair_sum = keep.astype(jnp.float32) + sibling.astype(jnp.float32)
    back = lax.all_to_all(pair_sum.astype(jnp.bfloat16), "sx", 0, 0, tiled=True)
    summed = jnp.sum(
        back.astype(jnp.float32).reshape((exp_local, chips // exp_local) + back.shape[1:]),
        axis=1,
    )
    summed = jnp.transpose(summed, (1, 0, 2, 3))
    returned = lax.all_to_all(
        summed.astype(jnp.bfloat16), TENSOR, split_axis=0, concat_axis=0, tiled=True
    ).astype(jnp.float32)
    moe_sum = jnp.dot(
        combine_table,
        returned.reshape(experts_all * capacity, width),
        preferred_element_type=jnp.float32,
        precision=lax.Precision.HIGHEST,
    )
    output = (mixed_rows.astype(jnp.float32) + moe_sum).astype(jnp.bfloat16)
    return (output, new_keys, new_values)


def solution(mesh):
    seq_size, tensor_size = mesh.devices.shape
    grid = Mesh(
        mesh.devices.reshape(seq_size // 2, 2, tensor_size // 2, 2), SEQ + TENSOR
    )
    return jax.shard_map(
        local,
        mesh=grid,
        in_specs=(
            P(SEQ + TENSOR, None),
            P(),
            P(None, None, TENSOR),
            P(TENSOR),
            P(TENSOR),
            P(TENSOR, None),
            P(SEQ, None, TENSOR),
            P(SEQ, None, TENSOR),
            P(),
            P(),
            P(),
            P(),
            P(SEQ + TENSOR, None),
            P(SEQ + TENSOR, None),
            P(TENSOR + SEQ, None, None),
            P(TENSOR + SEQ, None, None),
            P(TENSOR + SEQ, None, None),
        ),
        out_specs=(P(SEQ + TENSOR, None), P(SEQ, TENSOR), P(SEQ, TENSOR)),
        check_vma=False,
    )
```

```python
import jax
import jax.numpy as jnp
from jax import lax
from jax.sharding import Mesh
from jax.sharding import PartitionSpec as P

HD = 128
TOP = 8
EXP_DEV = 2
TENSOR = ("th", "tyl")
SEQ = ("sx", "sc")


def from_partner(value):
    return lax.ppermute(value, "tyl", [(0, 1), (1, 0)])


def passed_along(value, axis, by):
    devices = lax.axis_size(axis)
    pairs = [(i, i + by) for i in range(devices) if 0 <= i + by < devices]
    return lax.ppermute(value, axis, pairs)


def gather_by_exchange(value, axis):
    devices = lax.axis_size(axis)
    copies = jnp.broadcast_to(value[None], (devices,) + value.shape)
    got = lax.all_to_all(copies, axis, 0, 0, tiled=True)
    return got


def rms_scale(values, gain):
    mean_square = jnp.mean(values * values, axis=-1, keepdims=True)
    return values * lax.rsqrt(mean_square + 1e-05) * gain.astype(jnp.float32)


def attend_block(carry, queries_heads, block, mask):
    largest, total, accum = carry
    heads_local = queries_heads.shape[1]
    count = block.shape[0]
    key_block = block[:, 0].reshape(count, heads_local, HD)
    value_block = block[:, 1].reshape(count, heads_local, HD)
    scores = jnp.einsum(
        "qhd,khd->hqk", queries_heads, key_block, preferred_element_type=jnp.float32
    ) * HD ** (-0.5)
    scores = jnp.where(mask[None], scores, -1e30)
    new_largest = jnp.maximum(largest, jnp.max(scores, axis=-1))
    weights = jnp.where(mask[None], jnp.exp(scores - new_largest[:, :, None]), 0.0)
    factor = jnp.exp(largest - new_largest)
    total = total * factor + jnp.sum(weights, axis=-1)
    update = jnp.einsum(
        "hqk,khd->hqd",
        weights.astype(jnp.bfloat16),
        value_block,
        preferred_element_type=jnp.float32,
    )
    accum = accum * factor[:, :, None] + update
    return (new_largest, total, accum)


def local(
    tokens,
    attn_gain,
    w_qkv,
    q_gain,
    k_gain,
    w_out,
    prefix_keys,
    prefix_values,
    segments,
    request_group,
    prefix_owner,
    mlp_gain,
    expert_ids,
    gate_weights,
    w_gate,
    w_up,
    w_down,
):
    tensor_size = lax.axis_size(TENSOR)
    seq_size = lax.axis_size(SEQ)
    seq_index = lax.axis_index(SEQ)
    tensor_index = lax.axis_index(TENSOR)
    tok_dev = tokens.shape[0]
    width = tokens.shape[1]
    tok_seq = tok_dev * tensor_size
    columns = w_qkv.shape[2]
    lower_bit = tensor_index % 2
    prefix_own = jnp.stack([prefix_keys[0], prefix_values[0]], axis=1)
    prefix_partner = from_partner(prefix_own)
    prefix_full = jnp.where(
        lower_bit == 0,
        jnp.concatenate([prefix_own, prefix_partner], axis=-1),
        jnp.concatenate([prefix_partner, prefix_own], axis=-1),
    )
    piece = lax.all_gather(prefix_full[None], SEQ, axis=0, tiled=True)
    gains_in = from_partner(jnp.stack([q_gain, k_gain]))
    out_partner = from_partner(w_out)
    out_head = jnp.where(
        lower_bit == 0,
        jnp.concatenate([w_out, out_partner], axis=0),
        jnp.concatenate([out_partner, w_out], axis=0),
    )
    normed = rms_scale(tokens.astype(jnp.float32), attn_gain).astype(jnp.bfloat16)
    w_flat = w_qkv.reshape(width, 3 * columns)
    rows = gather_by_exchange(normed, TENSOR).reshape(tok_seq, width)
    projected = jnp.dot(
        rows,
        w_flat,
        preferred_element_type=jnp.float32,
    )
    query_part = projected[:, :columns]
    key_part = projected[:, columns : 2 * columns]
    value_part = projected[:, 2 * columns :]
    partial_squares = jnp.stack(
        [jnp.sum(query_part * query_part, axis=-1), jnp.sum(key_part * key_part, axis=-1)]
    )
    half_rows = tok_seq // 2
    row_blocks = half_rows // tok_dev

    def own_rows(values, mine=True):
        blocks = values.reshape((row_blocks, 2, tok_dev) + values.shape[1:])
        first, second = (blocks[:, 0], blocks[:, 1]) if mine else (blocks[:, 1], blocks[:, 0])
        return jnp.where(lower_bit == 0, first, second).reshape((half_rows,) + values.shape[1:])

    own_half = own_rows(query_part)
    send_half = own_rows(query_part, mine=False)
    raw_out = jnp.concatenate([send_half, key_part, value_part], axis=0)
    raw_out, partial_squares = lax.optimization_barrier((raw_out, partial_squares))
    raw_in = from_partner(raw_out)
    got_half = raw_in[:half_rows]
    got_keys = raw_in[half_rows : half_rows + tok_seq]
    got_values = raw_in[half_rows + tok_seq :]
    squares = jnp.sum(gather_by_exchange(partial_squares, TENSOR), axis=0)
    query_scale = lax.rsqrt(squares[0] / width + 1e-05)[:, None]
    key_scale = lax.rsqrt(squares[1] / width + 1e-05)[:, None]
    own_scale = own_rows(query_scale)
    own_query = (own_half * own_scale * q_gain.astype(jnp.float32)).astype(jnp.bfloat16)
    got_query = (got_half * own_scale * gains_in[0].astype(jnp.float32)).astype(jnp.bfloat16)
    new_keys = (key_part * key_scale * k_gain.astype(jnp.float32)).astype(jnp.bfloat16)
    new_values = value_part.astype(jnp.bfloat16)
    partner_keys = (got_keys * key_scale * gains_in[1].astype(jnp.float32)).astype(jnp.bfloat16)
    stacked = jnp.stack([new_keys, new_values], axis=1)
    partner = jnp.stack([partner_keys, got_values.astype(jnp.bfloat16)], axis=1)
    suffix_full = jnp.where(
        lower_bit == 0,
        jnp.concatenate([stacked, partner], axis=-1),
        jnp.concatenate([partner, stacked], axis=-1),
    )
    query_full = jnp.where(
        lower_bit == 0,
        jnp.concatenate([own_query, got_query], axis=-1),
        jnp.concatenate([got_query, own_query], axis=-1),
    )
    heads_local = 1
    queries_heads = query_full.reshape(half_rows, heads_local, HD)
    groups_count = prefix_owner.shape[0]
    request_count = request_group.shape[0]
    token_group = jnp.sum(
        jnp.where(
            segments[:, None] == jnp.arange(request_count, dtype=jnp.int32)[None, :],
            request_group[None, :],
            0,
        ),
        axis=1,
    )
    base_row = seq_index * tok_seq
    query_seg = own_rows(lax.dynamic_slice_in_dim(segments, base_row, tok_seq, 0))
    query_group = own_rows(lax.dynamic_slice_in_dim(token_group, base_row, tok_seq, 0))
    query_pos = own_rows(base_row + jnp.arange(tok_seq, dtype=jnp.int32))
    padded_seg = jnp.concatenate([jnp.full((tok_seq,), -1, jnp.int32), segments], axis=0)
    key_seg = lax.dynamic_slice_in_dim(padded_seg, base_row, 2 * tok_seq, 0)
    key_pos = base_row - tok_seq + jnp.arange(2 * tok_seq, dtype=jnp.int32)
    previous = passed_along(suffix_full, SEQ, 1)
    suffix_keys = jnp.concatenate([previous, suffix_full], axis=0)
    suffix_mask = (key_seg[None, :] == query_seg[:, None]) & (
        key_pos[None, :] <= query_pos[:, None]
    )
    carry = (
        jnp.full((heads_local, half_rows), -1e30, jnp.float32),
        jnp.zeros((heads_local, half_rows), jnp.float32),
        jnp.zeros((heads_local, half_rows, HD), jnp.float32),
    )
    carry = attend_block(carry, queries_heads, suffix_keys, suffix_mask)
    owner_of_query = jnp.sum(
        jnp.where(
            query_group[:, None] == jnp.arange(groups_count, dtype=jnp.int32)[None, :],
            prefix_owner[None, :],
            0,
        ),
        axis=1,
    )
    state = carry
    start = jnp.int32(0)
    for offset in range(piece.shape[0]):
        slot_mask = (owner_of_query == start + offset)[:, None]
        state = attend_block(state, queries_heads, piece[offset], slot_mask)
    carry = state
    attended = (carry[2] / carry[1][:, :, None]).astype(jnp.bfloat16)
    attended = jnp.transpose(attended, (1, 0, 2)).reshape(half_rows, heads_local * HD)
    attn_partial = jnp.dot(attended, out_head, preferred_element_type=jnp.float32)
    attn_partial = attn_partial.astype(jnp.bfloat16).reshape(row_blocks, tok_dev, width)
    attn_sum = jnp.sum(
        lax.all_to_all(attn_partial, "th", 0, 0, tiled=True).astype(jnp.float32), axis=0
    )
    mixed_rows = (tokens.astype(jnp.float32) + attn_sum).astype(jnp.bfloat16)
    expert_in = rms_scale(mixed_rows.astype(jnp.float32), mlp_gain).astype(jnp.bfloat16)
    exp_local = EXP_DEV
    experts_all = exp_local * tensor_size
    capacity = max(2, 2 * tok_dev * TOP // experts_all)
    flat_ids = expert_ids.reshape(-1)
    onehot = (flat_ids[:, None] == jnp.arange(experts_all, dtype=jnp.int32)[None, :]).astype(
        jnp.int32
    )
    before = jnp.cumsum(onehot, axis=0) - onehot
    slot = flat_ids * capacity + jnp.sum(before * onehot, axis=1)
    slot_match = (
        slot.reshape(tok_dev, TOP)[:, :, None]
        == jnp.arange(experts_all * capacity, dtype=jnp.int32)[None, None, :]
    )
    dispatch_table = jnp.transpose(jnp.any(slot_match, axis=1)).astype(jnp.bfloat16)
    combine_table = jnp.sum(jnp.where(slot_match, gate_weights[:, :, None], 0.0), axis=1)
    buffer = jnp.dot(dispatch_table, expert_in, preferred_element_type=jnp.float32).astype(
        jnp.bfloat16
    )
    buffer = buffer.reshape(tensor_size, exp_local, capacity, width)
    received = lax.all_to_all(buffer, TENSOR, split_axis=0, concat_axis=0, tiled=True)
    gate_local = w_gate[0]
    up_local = w_up[0]
    down_local = w_down[0]
    chips = lax.axis_size("sx")
    core = lax.axis_index("sc")
    per_expert = jnp.transpose(received, (1, 0, 2, 3))
    got = lax.all_to_all(
        jnp.repeat(per_expert, chips // exp_local, axis=0), "sx", 0, 0, tiled=True
    )
    from_sibling = lax.ppermute(got, "sc", [(0, 1), (1, 0)])
    chosen = jnp.where(
        core == 0, jnp.stack([got, from_sibling], axis=1), jnp.stack([from_sibling, got], axis=1)
    ).reshape((seq_size,) + got.shape[1:])
    gated = jnp.einsum("srcd,df->srcf", chosen, gate_local, preferred_element_type=jnp.float32)
    upward = jnp.einsum("srcd,df->srcf", chosen, up_local, preferred_element_type=jnp.float32)
    activity = (jax.nn.silu(gated) * upward).astype(jnp.bfloat16)
    result = jnp.einsum("srcf,fd->srcd", activity, down_local, preferred_element_type=jnp.float32)
    by_core = result.astype(jnp.bfloat16).reshape((chips, 2) + result.shape[1:])
    keep = jnp.where(core == 0, by_core[:, 0], by_core[:, 1])
    give = jnp.where(core == 0, by_core[:, 1], by_core[:, 0])
    sibling = lax.ppermute(give, "sc", [(0, 1), (1, 0)])
    pair_sum = keep.astype(jnp.float32) + sibling.astype(jnp.float32)
    back = lax.all_to_all(pair_sum.astype(jnp.bfloat16), "sx", 0, 0, tiled=True)
    summed = jnp.sum(
        back.astype(jnp.float32).reshape((exp_local, chips // exp_local) + back.shape[1:]),
        axis=1,
    )
    summed = jnp.transpose(summed, (1, 0, 2, 3))
    returned = lax.all_to_all(
        summed.astype(jnp.bfloat16), TENSOR, split_axis=0, concat_axis=0, tiled=True
    ).astype(jnp.float32)
    moe_sum = jnp.dot(
        combine_table,
        returned.reshape(experts_all * capacity, width),
        preferred_element_type=jnp.float32,
        precision=lax.Precision.HIGHEST,
    )
    output = (mixed_rows.astype(jnp.float32) + moe_sum).astype(jnp.bfloat16)
    return (output, new_keys, new_values)


def solution(mesh):
    seq_size, tensor_size = mesh.devices.shape
    grid = Mesh(
        mesh.devices.reshape(seq_size // 2, 2, tensor_size // 2, 2), SEQ + TENSOR
    )
    return jax.shard_map(
        local,
        mesh=grid,
        in_specs=(
            P(SEQ + TENSOR, None),
            P(),
            P(None, None, TENSOR),
            P(TENSOR),
            P(TENSOR),
            P(TENSOR, None),
            P(SEQ, None, TENSOR),
            P(SEQ, None, TENSOR),
            P(),
            P(),
            P(),
            P(),
            P(SEQ + TENSOR, None),
            P(SEQ + TENSOR, None),
            P(TENSOR + SEQ, None, None),
            P(TENSOR + SEQ, None, None),
            P(TENSOR + SEQ, None, None),
        ),
        out_specs=(P(SEQ + TENSOR, None), P(SEQ, TENSOR), P(SEQ, TENSOR)),
        check_vma=False,
    )
```

```python
import jax
import jax.numpy as jnp
from jax import lax
from jax.sharding import Mesh
from jax.sharding import PartitionSpec as P

HD = 128
TOP = 8
EXP_DEV = 2
TENSOR = ("th", "tyl")
SEQ = ("sx", "sc")


def from_partner(value):
    return lax.ppermute(value, "tyl", [(0, 1), (1, 0)])


def passed_along(value, axis, by):
    devices = lax.axis_size(axis)
    pairs = [(i, i + by) for i in range(devices) if 0 <= i + by < devices]
    return lax.ppermute(value, axis, pairs)


def gather_by_exchange(value, axis):
    devices = lax.axis_size(axis)
    copies = jnp.broadcast_to(value[None], (devices,) + value.shape)
    got = lax.all_to_all(copies, axis, 0, 0, tiled=True)
    return got


def rms_scale(values, gain):
    mean_square = jnp.mean(values * values, axis=-1, keepdims=True)
    return values * lax.rsqrt(mean_square + 1e-05) * gain.astype(jnp.float32)


def attend_block(carry, queries_heads, block, mask):
    largest, total, accum = carry
    heads_local = queries_heads.shape[1]
    count = block.shape[0]
    key_block = block[:, 0].reshape(count, heads_local, HD)
    value_block = block[:, 1].reshape(count, heads_local, HD)
    scores = jnp.einsum(
        "qhd,khd->hqk", queries_heads, key_block, preferred_element_type=jnp.float32
    ) * HD ** (-0.5)
    scores = jnp.where(mask[None], scores, -1e30)
    new_largest = jnp.maximum(largest, jnp.max(scores, axis=-1))
    weights = jnp.where(mask[None], jnp.exp(scores - new_largest[:, :, None]), 0.0)
    factor = jnp.exp(largest - new_largest)
    total = total * factor + jnp.sum(weights, axis=-1)
    update = jnp.einsum(
        "hqk,khd->hqd",
        weights.astype(jnp.bfloat16),
        value_block,
        preferred_element_type=jnp.float32,
    )
    accum = accum * factor[:, :, None] + update
    return (new_largest, total, accum)


def local(
    tokens,
    attn_gain,
    w_qkv,
    q_gain,
    k_gain,
    w_out,
    prefix_keys,
    prefix_values,
    segments,
    request_group,
    prefix_owner,
    mlp_gain,
    expert_ids,
    gate_weights,
    w_gate,
    w_up,
    w_down,
):
    tensor_size = lax.axis_size(TENSOR)
    seq_size = lax.axis_size(SEQ)
    seq_index = lax.axis_index(SEQ)
    tensor_index = lax.axis_index(TENSOR)
    tok_dev = tokens.shape[0]
    width = tokens.shape[1]
    tok_seq = tok_dev * tensor_size
    columns = w_qkv.shape[2]
    lower_bit = tensor_index % 2
    prefix_own = jnp.stack([prefix_keys[0], prefix_values[0]], axis=1)
    prefix_partner = from_partner(prefix_own)
    prefix_full = jnp.where(
        lower_bit == 0,
        jnp.concatenate([prefix_own, prefix_partner], axis=-1),
        jnp.concatenate([prefix_partner, prefix_own], axis=-1),
    )
    piece = lax.all_gather(prefix_full[None], SEQ, axis=0, tiled=True)
    gains_in = from_partner(jnp.stack([q_gain, k_gain]))
    out_partner = from_partner(w_out)
    out_head = jnp.where(
        lower_bit == 0,
        jnp.concatenate([w_out, out_partner], axis=0),
        jnp.concatenate([out_partner, w_out], axis=0),
    )

    def join(own, other, axis):
        return jnp.where(
            lower_bit == 0,
            jnp.concatenate([own, other], axis=axis),
            jnp.concatenate([other, own], axis=axis),
        )

    w_partner = from_partner(w_qkv)
    w_head = join(w_qkv, w_partner, 2)
    gains = join(jnp.stack([q_gain, k_gain]), gains_in, 1).astype(jnp.float32)
    normed = rms_scale(tokens.astype(jnp.float32), attn_gain).astype(jnp.bfloat16)
    half_rows = tok_seq // 2
    row_blocks = half_rows // tok_dev

    def own_rows(values, mine=True):
        blocks = values.reshape((row_blocks, 2, tok_dev) + values.shape[1:])
        first, second = (blocks[:, 0], blocks[:, 1]) if mine else (blocks[:, 1], blocks[:, 0])
        return jnp.where(lower_bit == 0, first, second).reshape((half_rows,) + values.shape[1:])

    rows = gather_by_exchange(normed, "th").reshape(half_rows, width)
    projected = jnp.dot(
        rows, w_head.reshape(width, 3 * 2 * columns), preferred_element_type=jnp.float32
    ).reshape(half_rows, 3, 2 * columns)
    query_part = projected[:, 0]
    key_part = projected[:, 1]
    partial_squares = jnp.stack(
        [jnp.sum(query_part * query_part, axis=-1), jnp.sum(key_part * key_part, axis=-1)]
    )
    squares = jnp.sum(gather_by_exchange(partial_squares, "th"), axis=0)
    query_full = (
        query_part * lax.rsqrt(squares[0] / width + 1e-05)[:, None] * gains[0]
    ).astype(jnp.bfloat16)
    own_keys = (
        key_part * lax.rsqrt(squares[1] / width + 1e-05)[:, None] * gains[1]
    ).astype(jnp.bfloat16)
    own_kv = jnp.stack([own_keys, projected[:, 2].astype(jnp.bfloat16)], axis=1)
    other_kv = from_partner(own_kv)
    kv_blocks = (row_blocks, 1, tok_dev, 2, 2 * columns)
    suffix_full = join(own_kv.reshape(kv_blocks), other_kv.reshape(kv_blocks), 1).reshape(
        tok_seq, 2, 2 * columns
    )
    own_cols = jnp.where(lower_bit == 0, suffix_full[..., :columns], suffix_full[..., columns:])
    new_keys = own_cols[:, 0]
    new_values = own_cols[:, 1]
    heads_local = 1
    queries_heads = query_full.reshape(half_rows, heads_local, HD)
    groups_count = prefix_owner.shape[0]
    request_count = request_group.shape[0]
    token_group = jnp.sum(
        jnp.where(
            segments[:, None] == jnp.arange(request_count, dtype=jnp.int32)[None, :],
            request_group[None, :],
            0,
        ),
        axis=1,
    )
    base_row = seq_index * tok_seq
    query_seg = own_rows(lax.dynamic_slice_in_dim(segments, base_row, tok_seq, 0))
    query_group = own_rows(lax.dynamic_slice_in_dim(token_group, base_row, tok_seq, 0))
    query_pos = own_rows(base_row + jnp.arange(tok_seq, dtype=jnp.int32))
    padded_seg = jnp.concatenate([jnp.full((tok_seq,), -1, jnp.int32), segments], axis=0)
    key_seg = lax.dynamic_slice_in_dim(padded_seg, base_row, 2 * tok_seq, 0)
    key_pos = base_row - tok_seq + jnp.arange(2 * tok_seq, dtype=jnp.int32)
    previous = passed_along(suffix_full, SEQ, 1)
    suffix_keys = jnp.concatenate([previous, suffix_full], axis=0)
    suffix_mask = (key_seg[None, :] == query_seg[:, None]) & (
        key_pos[None, :] <= query_pos[:, None]
    )
    carry = (
        jnp.full((heads_local, half_rows), -1e30, jnp.float32),
        jnp.zeros((heads_local, half_rows), jnp.float32),
        jnp.zeros((heads_local, half_rows, HD), jnp.float32),
    )
    carry = attend_block(carry, queries_heads, suffix_keys, suffix_mask)
    owner_of_query = jnp.sum(
        jnp.where(
            query_group[:, None] == jnp.arange(groups_count, dtype=jnp.int32)[None, :],
            prefix_owner[None, :],
            0,
        ),
        axis=1,
    )
    state = carry
    start = jnp.int32(0)
    for offset in range(piece.shape[0]):
        slot_mask = (owner_of_query == start + offset)[:, None]
        state = attend_block(state, queries_heads, piece[offset], slot_mask)
    carry = state
    attended = (carry[2] / carry[1][:, :, None]).astype(jnp.bfloat16)
    attended = jnp.transpose(attended, (1, 0, 2)).reshape(half_rows, heads_local * HD)
    attn_partial = jnp.dot(attended, out_head, preferred_element_type=jnp.float32)
    attn_partial = attn_partial.astype(jnp.bfloat16).reshape(row_blocks, tok_dev, width)
    attn_sum = jnp.sum(
        lax.all_to_all(attn_partial, "th", 0, 0, tiled=True).astype(jnp.float32), axis=0
    )
    mixed_rows = (tokens.astype(jnp.float32) + attn_sum).astype(jnp.bfloat16)
    expert_in = rms_scale(mixed_rows.astype(jnp.float32), mlp_gain).astype(jnp.bfloat16)
    exp_local = EXP_DEV
    experts_all = exp_local * tensor_size
    capacity = max(2, 2 * tok_dev * TOP // experts_all)
    flat_ids = expert_ids.reshape(-1)
    onehot = (flat_ids[:, None] == jnp.arange(experts_all, dtype=jnp.int32)[None, :]).astype(
        jnp.int32
    )
    before = jnp.cumsum(onehot, axis=0) - onehot
    slot = flat_ids * capacity + jnp.sum(before * onehot, axis=1)
    slot_match = (
        slot.reshape(tok_dev, TOP)[:, :, None]
        == jnp.arange(experts_all * capacity, dtype=jnp.int32)[None, None, :]
    )
    dispatch_table = jnp.transpose(jnp.any(slot_match, axis=1)).astype(jnp.bfloat16)
    combine_table = jnp.sum(jnp.where(slot_match, gate_weights[:, :, None], 0.0), axis=1)
    buffer = jnp.dot(dispatch_table, expert_in, preferred_element_type=jnp.float32).astype(
        jnp.bfloat16
    )
    buffer = buffer.reshape(tensor_size, exp_local, capacity, width)
    received = lax.all_to_all(buffer, TENSOR, split_axis=0, concat_axis=0, tiled=True)
    gate_local = w_gate[0]
    up_local = w_up[0]
    down_local = w_down[0]
    chips = lax.axis_size("sx")
    core = lax.axis_index("sc")
    per_expert = jnp.transpose(received, (1, 0, 2, 3))
    got = lax.all_to_all(
        jnp.repeat(per_expert, chips // exp_local, axis=0), "sx", 0, 0, tiled=True
    )
    from_sibling = lax.ppermute(got, "sc", [(0, 1), (1, 0)])
    chosen = jnp.where(
        core == 0, jnp.stack([got, from_sibling], axis=1), jnp.stack([from_sibling, got], axis=1)
    ).reshape((seq_size,) + got.shape[1:])
    gated = jnp.einsum("srcd,df->srcf", chosen, gate_local, preferred_element_type=jnp.float32)
    upward = jnp.einsum("srcd,df->srcf", chosen, up_local, preferred_element_type=jnp.float32)
    activity = (jax.nn.silu(gated) * upward).astype(jnp.bfloat16)
    result = jnp.einsum("srcf,fd->srcd", activity, down_local, preferred_element_type=jnp.float32)
    by_core = result.astype(jnp.bfloat16).reshape((chips, 2) + result.shape[1:])
    keep = jnp.where(core == 0, by_core[:, 0], by_core[:, 1])
    give = jnp.where(core == 0, by_core[:, 1], by_core[:, 0])
    sibling = lax.ppermute(give, "sc", [(0, 1), (1, 0)])
    pair_sum = keep.astype(jnp.float32) + sibling.astype(jnp.float32)
    back = lax.all_to_all(pair_sum.astype(jnp.bfloat16), "sx", 0, 0, tiled=True)
    summed = jnp.sum(
        back.astype(jnp.float32).reshape((exp_local, chips // exp_local) + back.shape[1:]),
        axis=1,
    )
    summed = jnp.transpose(summed, (1, 0, 2, 3))
    returned = lax.all_to_all(
        summed.astype(jnp.bfloat16), TENSOR, split_axis=0, concat_axis=0, tiled=True
    ).astype(jnp.float32)
    moe_sum = jnp.dot(
        combine_table,
        returned.reshape(experts_all * capacity, width),
        preferred_element_type=jnp.float32,
        precision=lax.Precision.HIGHEST,
    )
    output = (mixed_rows.astype(jnp.float32) + moe_sum).astype(jnp.bfloat16)
    return (output, new_keys, new_values)


def solution(mesh):
    seq_size, tensor_size = mesh.devices.shape
    grid = Mesh(
        mesh.devices.reshape(seq_size // 2, 2, tensor_size // 2, 2), SEQ + TENSOR
    )
    return jax.shard_map(
        local,
        mesh=grid,
        in_specs=(
            P(SEQ + TENSOR, None),
            P(),
            P(None, None, TENSOR),
            P(TENSOR),
            P(TENSOR),
            P(TENSOR, None),
            P(SEQ, None, TENSOR),
            P(SEQ, None, TENSOR),
            P(),
            P(),
            P(),
            P(),
            P(SEQ + TENSOR, None),
            P(SEQ + TENSOR, None),
            P(TENSOR + SEQ, None, None),
            P(TENSOR + SEQ, None, None),
            P(TENSOR + SEQ, None, None),
        ),
        out_specs=(P(SEQ + TENSOR, None), P(SEQ, TENSOR), P(SEQ, TENSOR)),
        check_vma=False,
    )
```
